32 devices in a mesh: group: 2 (over x), dev: 16 (over z, y, core).
Axes of the slice: x: 2, y: 2, z: 4, core: 2. Of those that a mesh axis runs over, the one named last changes fastest.
Arguments:
- suffix_x: bfloat16 [2, 4096, 1600], P('group', 'dev'), may hold values from -6 to 6
- suffix_query: bfloat16 [2, 4096, 1024], P('group', 'dev'), may hold values from -128 to 128
- suffix_keyval: bfloat16 [2, 4096, 2048], P('group', 'dev'), may hold values from -6 to 6
- prefix_keyval: bfloat16 [2, 128, 2048], P('group', 'dev'), may hold values from -6 to 6
- prefix_hidden: bfloat16 [2, 128, 1600], P('group', 'dev'), may hold values from -6 to 6
- kv_weight: bfloat16 [1600, 2048], replicated, may hold values from -0.15625 to 0.15625
- out_weight: bfloat16 [1024, 1600], replicated, may hold values from -0.1875 to 0.1875
- fc_weight: bfloat16 [1600, 3840], P(None, ('group', 'dev')), may hold values from -0.15625 to 0.15625
- proj_weight: bfloat16 [3840, 1600], P(('group', 'dev')), may hold values from -0.09375 to 0.09375
- lengths: int32 [2, 16], P('group'), may hold values from 1 to 256, 2048 in all within a row
- placement: int32 [2, 16], P('group'), may hold values from 0 to 15, each once within a row
- owners: int32 [2, 16], P('group'), may hold values from 0 to 15, each once within a row
- recompute: int32 [2, 2], P('group'), may hold values from 0 to 15
Outputs:
- layer_out: bfloat16 [2, 4096, 1600], P('group', 'dev')
The draws below stay inside these ranges and needn't reach their ends.
All inputs are finite; a program needn't handle non-finite values.
Results may differ from the reference program's by a relative error of at most 0.008.
Values may be sent and summed in bfloat16 or wider, within the bound.
No kernel may reach another device: no remote copies, remote signals or barrier semaphores. Data moves between devices by JAX's collectives and lax.ppermute only.
A program may use at most 128 MiB of HBM per device.

```python
import math
import jax
import jax.numpy as jnp
import numpy as np
from jax import lax

D = 1600
HEADS = 16
HEAD_DIM = 64
FFW = 3840
CAP = 256
PBLK = 8
ATT = 1024
GROUPS = 2
NBLK = 16
PREFIX = 128
REC = 2
N_DEV = 16


def draw_suffix_query(key, part):
    first_key = jax.random.fold_in(key, 0)
    row_count = N_DEV * CAP
    drawn_draw = jax.random.normal(first_key, (GROUPS, row_count, ATT), jnp.float32)
    return (3.0 * jnp.clip(drawn_draw, -6.0, 6.0)).astype(jnp.bfloat16)


def place_ends(array, rng, least, top_value):
    index_at = [jax.random.randint(jax.random.fold_in(rng, axis), (), 0, length) for axis, length in enumerate(array.shape)]
    main_axis = array.shape.index(max(array.shape))
    neighbour = index_at[:main_axis] + [(index_at[main_axis] + 1) % array.shape[main_axis]] + index_at[main_axis + 1:]
    return array.at[tuple(index_at)].set(least).at[tuple(neighbour)].set(top_value)


def levels(stream_key, extent, shards, least, top_value):
    def one(dim, shards_of):
        steps = jax.random.uniform(jax.random.fold_in(jax.random.fold_in(stream_key, 6), dim), (shards_of,), jnp.float32, least / len(shards), top_value / len(shards))
        return jnp.repeat(jnp.exp(steps), extent[dim] // shards_of).reshape((-1,) + (1,) * (len(extent) - dim - 1))

    gain = one(*shards[0])
    for cut in shards[1:]:
        gain = gain * one(*cut)
    return gain


def split_up(number_of, total, reach, lean):
    loads = [(1 << 20) // math.isqrt(standing ** lean) + 1 for standing in range(2, number_of + 1)]
    spare, given = total - reach - (number_of - 1), [1] * (number_of - 1)
    while spare > 0:
        free = [i for i in range(number_of - 1) if given[i] < reach]
        pool, budget = sum([loads[i] for i in free]), spare
        for i in free:
            extra = min(reach - given[i], max(1, budget * loads[i] // pool), spare)
            given[i] = given[i] + extra
            spare = spare - extra
    return np.array([reach] + given)


def uneven(rng, number_of, total, most, lean):
    if number_of == 2:
        one = jax.random.randint(rng, (), max(1, total - most), min(most, total - 1) + 1)
        return jnp.stack([one, total - one])
    sizes = jnp.asarray(split_up(number_of, total, most, lean), jnp.int32)
    couples = (number_of - 1) // 2
    source_of, sink = sizes[1:1 + 2 * couples:2], sizes[2:2 + 2 * couples:2]
    room = jnp.minimum(source_of - 1, most - sink)
    moved = jax.random.randint(jax.random.fold_in(rng, 1), (couples,), 0, 1 << 20) % (room + 1)
    sizes = sizes.at[1:1 + 2 * couples:2].set(source_of - moved).at[2:2 + 2 * couples:2].set(sink + moved)
    return sizes[jax.random.permutation(jax.random.fold_in(rng, 2), number_of)]


def gaussian(own_key, shape, deviation, bound, pieces=(), kind=jnp.bfloat16):
    level = levels(own_key, shape, pieces, -0.22, 0.18) if pieces else 1.0
    drawn = jax.random.normal(own_key, shape, jnp.float32) * deviation * level
    return jnp.minimum(jnp.maximum(drawn, -bound), bound).astype(kind)


def setup_inputs(seed: int = 0) -> dict:
    keys = jax.random.split(jax.random.key(seed), 14)
    suffix_x = gaussian(keys[0], (GROUPS, N_DEV * CAP, D), 1.0, 6.0, ((0, 2), (1, 16)))
    suffix_query = draw_suffix_query(jax.random.fold_in(keys[13], 71), 0)
    suffix_keyval = gaussian(keys[2], (GROUPS, N_DEV * CAP, 2 * ATT), 1.0, 6.0, ((0, 2), (1, 16)))
    prefix_keyval = gaussian(keys[3], (GROUPS, PREFIX, 2 * ATT), 1.0, 6.0, ((0, 2), (1, 16)))
    prefix_hidden = gaussian(keys[4], (GROUPS, PREFIX, D), 1.0, 6.0, ((0, 2), (1, 16)))
    kv_weight = gaussian(keys[5], (D, 2 * ATT), D ** -0.5, 0.15625)
    out_weight = gaussian(keys[6], (ATT, D), ATT ** -0.5, 0.1875)
    fc_weight = gaussian(keys[7], (D, FFW), D ** -0.5, 0.15625, ((1, 32),))
    proj_weight = gaussian(keys[8], (FFW, D), FFW ** -0.5, 0.09375, ((0, 32),))
    lengths = jax.vmap(lambda own: uneven(own, N_DEV, CAP * N_DEV // 2, CAP, 2))(jax.random.split(keys[9], GROUPS)).reshape((GROUPS, N_DEV)).astype(jnp.int32)
    placement = jax.vmap(lambda own: jax.random.permutation(own, N_DEV))(jax.random.split(keys[10], GROUPS)).reshape((GROUPS, N_DEV)).astype(jnp.int32)
    owners = jax.vmap(lambda own: jax.random.permutation(own, NBLK))(jax.random.split(keys[11], GROUPS)).reshape((GROUPS, NBLK)).astype(jnp.int32)
    recompute = place_ends(jax.random.randint(keys[12], (GROUPS, REC), 0, NBLK), jax.random.fold_in(keys[12], 1), 0, NBLK - 1).astype(jnp.int32)
    return dict(suffix_x=suffix_x, suffix_query=suffix_query, suffix_keyval=suffix_keyval, prefix_keyval=prefix_keyval, prefix_hidden=prefix_hidden, kv_weight=kv_weight, out_weight=out_weight, fc_weight=fc_weight, proj_weight=proj_weight, lengths=lengths, placement=placement, owners=owners, recompute=recompute)


NEGATIVE = -1e+30
EPSILON = 1e-05
SCORE_SCALE = 0.125

def normalize(values_in):
    values_in = values_in.astype(jnp.float32)
    average = lax.optimization_barrier(jnp.mean(values_in, axis=-1, keepdims=True))
    centered = values_in - average
    variance = lax.optimization_barrier(jnp.mean(centered * centered, axis=-1, keepdims=True))
    return centered / jnp.sqrt(variance + EPSILON)

def reference(suffix_x, suffix_query, suffix_keyval, prefix_keyval, prefix_hidden, kv_weight, out_weight, fc_weight, proj_weight, lengths, placement, owners, recompute):
    device_ids = jnp.arange(N_DEV, dtype=jnp.int32)
    positions = jnp.arange(CAP, dtype=jnp.int32)
    results = []
    for group_id in range(GROUPS):
        hits = placement[group_id][:, None] == device_ids[None, :]
        device_length = lax.optimization_barrier(jnp.sum(jnp.where(hits, lengths[group_id][:, None], 0), axis=0)).astype(jnp.int32)
        chosen_owner = owners[group_id][recompute[group_id]]
        stale_device = jnp.any(chosen_owner[:, None] == device_ids[None, :], axis=0)
        stale_rows = jnp.repeat(stale_device, PBLK)
        normed_prefix = normalize(prefix_hidden[group_id]).astype(jnp.bfloat16)
        fresh = jnp.dot(normed_prefix, kv_weight, preferred_element_type=jnp.float32).astype(jnp.bfloat16)
        prefix_rows = jnp.where(stale_rows[:, None], fresh, prefix_keyval[group_id])
        prefix_key = prefix_rows[:, :ATT].reshape(PREFIX, HEADS, HEAD_DIM)
        prefix_val = prefix_rows[:, ATT:].reshape(PREFIX, HEADS, HEAD_DIM)

        def one_device(device_id):
            first_row = (device_id * CAP).astype(jnp.int32)
            queries = lax.dynamic_slice_in_dim(suffix_query[group_id], first_row, CAP, 0).reshape(CAP, HEADS, HEAD_DIM)
            own_rows = lax.dynamic_slice_in_dim(suffix_keyval[group_id], first_row, CAP, 0)
            key_rows = jnp.concatenate([prefix_key, own_rows[:, :ATT].reshape(CAP, HEADS, HEAD_DIM)], axis=0)
            val_rows = jnp.concatenate([prefix_val, own_rows[:, ATT:].reshape(CAP, HEADS, HEAD_DIM)], axis=0)
            scores = jnp.einsum('qhd,khd->hqk', queries.astype(jnp.float32), key_rows.astype(jnp.float32)) * SCORE_SCALE
            my_length = device_length[device_id]
            causal = (positions[None, :] <= positions[:, None]) & (positions[None, :] < my_length)
            allowed = jnp.concatenate([jnp.ones((CAP, PREFIX), dtype=bool), causal], axis=1)
            scores = jnp.where(allowed[None], scores, NEGATIVE)
            row_top = lax.optimization_barrier(jnp.max(scores, axis=-1, keepdims=True))
            weights = jnp.where(allowed[None], jnp.exp(scores - row_top), 0.0)
            total = lax.optimization_barrier(jnp.sum(weights, axis=-1))
            weights_low = weights.astype(jnp.bfloat16)
            mixed = jnp.einsum('hqk,khd->qhd', weights_low.astype(jnp.float32), val_rows.astype(jnp.float32))
            attended = (mixed / jnp.transpose(total)[:, :, None]).reshape(CAP, ATT).astype(jnp.bfloat16)
            residual = lax.dynamic_slice_in_dim(suffix_x[group_id], first_row, CAP, 0).astype(jnp.float32)
            residual = residual + jnp.dot(attended, out_weight, preferred_element_type=jnp.float32)
            normed = normalize(residual).astype(jnp.bfloat16)
            inner = jnp.dot(normed, fc_weight, preferred_element_type=jnp.float32)
            activated = jax.nn.gelu(inner, approximate=True).astype(jnp.bfloat16)
            feed_out = jnp.dot(activated, proj_weight, preferred_element_type=jnp.float32)
            live = positions[:, None] < my_length
            return jnp.where(live, residual + feed_out, 0.0).astype(jnp.bfloat16)
        blocks = lax.map(one_device, device_ids)
        results.append(blocks.reshape(N_DEV * CAP, D))
    return jnp.stack(results, axis=0)
```

```python
import jax
import jax.numpy as jnp
from jax import lax
from jax.sharding import Mesh, PartitionSpec as P

HEAD_DIM = 64


NEGATIVE = -1e30
EPSILON = 1e-05
SCORE_SCALE = 0.125


def normalize(values_in):
    values_in = values_in.astype(jnp.float32)
    average = jnp.mean(values_in, axis=-1, keepdims=True)
    centered = values_in - average
    variance = jnp.mean(centered * centered, axis=-1, keepdims=True)
    return centered / jnp.sqrt(variance + EPSILON)


def absorb(state, queries, keyval, allowed):
    running_top, running_total, accumulated = state
    head_count = queries.shape[1]
    head_size = queries.shape[2]
    row_count = keyval.shape[0]
    width_att = head_count * head_size
    key_rows = keyval[:, :width_att].reshape(row_count, head_count, head_size)
    val_rows = keyval[:, width_att:].reshape(row_count, head_count, head_size)
    scores = (
        jnp.einsum("qhd,khd->hqk", queries, key_rows, preferred_element_type=jnp.float32)
        * SCORE_SCALE
    )
    scores = jnp.where(allowed[None], scores, NEGATIVE)
    new_top = jnp.maximum(running_top, jnp.max(scores, axis=-1))
    factor = jnp.exp(running_top - new_top)
    weights = jnp.where(allowed[None], jnp.exp(scores - new_top[:, :, None]), 0.0)
    running_total = running_total * factor + jnp.sum(weights, axis=-1)
    weights_low = weights.astype(jnp.bfloat16)
    update = jnp.einsum("hqk,khd->qhd", weights_low, val_rows, preferred_element_type=jnp.float32)
    accumulated = accumulated * jnp.transpose(factor)[:, :, None] + update
    return (new_top, running_total, accumulated)


def per_device(
    suffix_x,
    suffix_query,
    suffix_keyval,
    prefix_keyval,
    prefix_hidden,
    kv_weight,
    out_weight,
    fc_weight,
    proj_weight,
    lengths,
    placement,
    owners,
    recompute,
):
    device_count = lax.axis_size("chip") * lax.axis_size("core")
    my_device = lax.axis_index("chip") * lax.axis_size("core") + lax.axis_index("core")
    slots = suffix_x.shape[1]
    block_rows = prefix_keyval.shape[1]
    width_att = suffix_query.shape[2]
    head_count = width_att // HEAD_DIM
    device_ids = jnp.arange(device_count, dtype=jnp.int32)
    hits = placement[0][:, None] == device_ids[None, :]
    device_length = jnp.sum(jnp.where(hits, lengths[0][:, None], 0), axis=0)
    my_length = jnp.sum(jnp.where(device_ids == my_device, device_length, 0))
    block_ids = jnp.arange(owners.shape[1], dtype=jnp.int32)
    chosen = recompute[0]
    chosen_owner = jnp.sum(
        jnp.where(chosen[:, None] == block_ids[None, :], owners[0][None, :], 0), axis=1
    )
    stale_device = jnp.any(chosen_owner[:, None] == device_ids[None, :], axis=0)
    queries = suffix_query[0].reshape(slots, head_count, HEAD_DIM)
    normed_prefix = normalize(prefix_hidden[0]).astype(jnp.bfloat16)
    fresh = jnp.dot(normed_prefix, kv_weight, preferred_element_type=jnp.float32).astype(
        jnp.bfloat16
    )
    my_stale = jnp.any(chosen_owner == my_device)
    local_kv = jnp.where(my_stale, fresh, prefix_keyval[0])
    skip_device = jnp.zeros_like(stale_device)
    gathered = lax.all_gather(local_kv, ("chip", "core"), axis=0, tiled=True)
    prefix_count = gathered.shape[0]
    row_device = jnp.arange(prefix_count, dtype=jnp.int32) // block_rows
    skipped = jnp.any((row_device[:, None] == device_ids[None, :]) & skip_device[None, :], axis=1)
    state = (
        jnp.full((head_count, slots), NEGATIVE, jnp.float32),
        jnp.zeros((head_count, slots), jnp.float32),
        jnp.zeros((slots, head_count, HEAD_DIM), jnp.float32),
    )
    key_block = 512 if prefix_count % 512 == 0 else prefix_count
    for block_start in range(0, prefix_count, key_block):
        kept = jnp.logical_not(skipped[block_start : block_start + key_block])
        allowed = jnp.broadcast_to(kept[None, :], (slots, key_block))
        state = absorb(state, queries, gathered[block_start : block_start + key_block], allowed)
    positions = jnp.arange(slots, dtype=jnp.int32)
    causal = (positions[None, :] <= positions[:, None]) & (positions[None, :] < my_length)
    state = absorb(state, queries, suffix_keyval[0], causal)
    final_top, final_total, accumulated = state
    attended = (
        (accumulated / jnp.transpose(final_total)[:, :, None])
        .reshape(slots, width_att)
        .astype(jnp.bfloat16)
    )
    projected = jnp.dot(attended, out_weight, preferred_element_type=jnp.float32)
    residual = suffix_x[0].astype(jnp.float32) + projected
    normed = normalize(residual).astype(jnp.bfloat16)
    fc_part, proj_part = (
        lax.all_gather(fc_weight, ("group", "chip"), axis=1, tiled=True),
        lax.all_gather(proj_weight, ("group", "chip"), axis=0, tiled=True),
    )
    normed_pair = lax.all_gather(normed, "core", axis=0, tiled=True)
    inner = jnp.dot(normed_pair, fc_part, preferred_element_type=jnp.float32)
    activated = jax.nn.gelu(inner, approximate=True).astype(jnp.bfloat16)
    feed_pair = jnp.dot(activated, proj_part, preferred_element_type=jnp.float32)
    feed_out = lax.psum_scatter(feed_pair, "core", scatter_dimension=0, tiled=True)
    live = positions[:, None] < my_length
    return jnp.where(live, residual + feed_out, 0.0).astype(jnp.bfloat16)[None]


def solution(mesh):
    group_count, device_count = mesh.devices.shape
    split = Mesh(
        mesh.devices.reshape(group_count, device_count // 2, 2), ("group", "chip", "core")
    )
    rows = ("chip", "core")
    return jax.shard_map(
        per_device,
        mesh=split,
        in_specs=(
            P("group", rows, None),
            P("group", rows, None),
            P("group", rows, None),
            P("group", rows, None),
            P("group", rows, None),
            P(),
            P(),
            P(None, ("group", "chip", "core")),
            P(("group", "chip", "core"), None),
            P("group", None),
            P("group", None),
            P("group", None),
            P("group", None),
        ),
        out_specs=P("group", rows, None),
        check_vma=False,
    )
```

```python
import jax
import jax.numpy as jnp
from jax import lax
from jax.sharding import PartitionSpec as P

HEAD_DIM = 64


NEGATIVE = -1e30
EPSILON = 1e-05
SCORE_SCALE = 0.125


def normalize(values_in):
    values_in = values_in.astype(jnp.float32)
    average = jnp.mean(values_in, axis=-1, keepdims=True)
    centered = values_in - average
    variance = jnp.mean(centered * centered, axis=-1, keepdims=True)
    return centered / jnp.sqrt(variance + EPSILON)


def absorb(state, queries, keyval, allowed):
    running_top, running_total, accumulated = state
    head_count = queries.shape[1]
    head_size = queries.shape[2]
    row_count = keyval.shape[0]
    width_att = head_count * head_size
    key_rows = keyval[:, :width_att].reshape(row_count, head_count, head_size)
    val_rows = keyval[:, width_att:].reshape(row_count, head_count, head_size)
    scores = (
        jnp.einsum("qhd,khd->hqk", queries, key_rows, preferred_element_type=jnp.float32)
        * SCORE_SCALE
    )
    scores = jnp.where(allowed[None], scores, NEGATIVE)
    new_top = jnp.maximum(running_top, jnp.max(scores, axis=-1))
    factor = jnp.exp(running_top - new_top)
    weights = jnp.where(allowed[None], jnp.exp(scores - new_top[:, :, None]), 0.0)
    running_total = running_total * factor + jnp.sum(weights, axis=-1)
    weights_low = weights.astype(jnp.bfloat16)
    update = jnp.einsum("hqk,khd->qhd", weights_low, val_rows, preferred_element_type=jnp.float32)
    accumulated = accumulated * jnp.transpose(factor)[:, :, None] + update
    return (new_top, running_total, accumulated)


def per_device(
    suffix_x,
    suffix_query,
    suffix_keyval,
    prefix_keyval,
    prefix_hidden,
    kv_weight,
    out_weight,
    fc_weight,
    proj_weight,
    lengths,
    placement,
    owners,
    recompute,
):
    device_count = lax.axis_size("dev")
    my_device = lax.axis_index("dev")
    slots = suffix_x.shape[1]
    block_rows = prefix_keyval.shape[1]
    width_att = suffix_query.shape[2]
    head_count = width_att // HEAD_DIM
    device_ids = jnp.arange(device_count, dtype=jnp.int32)
    hits = placement[0][:, None] == device_ids[None, :]
    device_length = jnp.sum(jnp.where(hits, lengths[0][:, None], 0), axis=0)
    my_length = jnp.sum(jnp.where(device_ids == my_device, device_length, 0))
    block_ids = jnp.arange(owners.shape[1], dtype=jnp.int32)
    chosen = recompute[0]
    chosen_owner = jnp.sum(
        jnp.where(chosen[:, None] == block_ids[None, :], owners[0][None, :], 0), axis=1
    )
    stale_device = jnp.any(chosen_owner[:, None] == device_ids[None, :], axis=0)
    queries = suffix_query[0].reshape(slots, head_count, HEAD_DIM)
    normed_prefix = normalize(prefix_hidden[0]).astype(jnp.bfloat16)
    fresh = jnp.dot(normed_prefix, kv_weight, preferred_element_type=jnp.float32).astype(
        jnp.bfloat16
    )
    my_stale = jnp.any(chosen_owner == my_device)
    local_kv = jnp.where(my_stale, fresh, prefix_keyval[0])
    skip_device = jnp.zeros_like(stale_device)
    gathered = lax.all_gather(local_kv, "dev", axis=0, tiled=True)
    prefix_count = gathered.shape[0]
    row_device = jnp.arange(prefix_count, dtype=jnp.int32) // block_rows
    skipped = jnp.any((row_device[:, None] == device_ids[None, :]) & skip_device[None, :], axis=1)
    state = (
        jnp.full((head_count, slots), NEGATIVE, jnp.float32),
        jnp.zeros((head_count, slots), jnp.float32),
        jnp.zeros((slots, head_count, HEAD_DIM), jnp.float32),
    )
    key_block = 512 if prefix_count % 512 == 0 else prefix_count
    for block_start in range(0, prefix_count, key_block):
        kept = jnp.logical_not(skipped[block_start : block_start + key_block])
        allowed = jnp.broadcast_to(kept[None, :], (slots, key_block))
        state = absorb(state, queries, gathered[block_start : block_start + key_block], allowed)
    positions = jnp.arange(slots, dtype=jnp.int32)
    causal = (positions[None, :] <= positions[:, None]) & (positions[None, :] < my_length)
    state = absorb(state, queries, suffix_keyval[0], causal)
    final_top, final_total, accumulated = state
    attended = (
        (accumulated / jnp.transpose(final_total)[:, :, None])
        .reshape(slots, width_att)
        .astype(jnp.bfloat16)
    )
    projected = jnp.dot(attended, out_weight, preferred_element_type=jnp.float32)
    residual = suffix_x[0].astype(jnp.float32) + projected
    normed = normalize(residual).astype(jnp.bfloat16)
    hidden_part = fc_weight.shape[1]
    both = jnp.concatenate([fc_weight.T, proj_weight], axis=0)
    both_full = lax.all_gather(both, ("group", "dev"), axis=0)
    fc_rows = both_full[:, :hidden_part].reshape(-1, both.shape[1])
    proj_full = both_full[:, hidden_part:].reshape(-1, both.shape[1])
    inner = lax.dot_general(
        normed, fc_rows, (((1,), (1,)), ((), ())), preferred_element_type=jnp.float32
    )
    activated = jax.nn.gelu(inner, approximate=True).astype(jnp.bfloat16)
    feed_out = jnp.dot(activated, proj_full, preferred_element_type=jnp.float32)
    live = positions[:, None] < my_length
    return jnp.where(live, residual + feed_out, 0.0).astype(jnp.bfloat16)[None]


def solution(mesh):
    return jax.shard_map(
        per_device,
        mesh=mesh,
        in_specs=(
            P("group", "dev", None),
            P("group", "dev", None),
            P("group", "dev", None),
            P("group", "dev", None),
            P("group", "dev", None),
            P(),
            P(),
            P(None, ("group", "dev")),
            P(("group", "dev"), None),
            P("group", None),
            P("group", None),
            P("group", None),
            P("group", None),
        ),
        out_specs=P("group", "dev", None),
        check_vma=False,
    )
```

```python
import jax
import jax.numpy as jnp
from jax import lax
from jax.sharding import PartitionSpec as P

HEAD_DIM = 64


NEGATIVE = -1e30
EPSILON = 1e-05
SCORE_SCALE = 0.125


def normalize(values_in):
    values_in = values_in.astype(jnp.float32)
    average = jnp.mean(values_in, axis=-1, keepdims=True)
    centered = values_in - average
    variance = jnp.mean(centered * centered, axis=-1, keepdims=True)
    return centered / jnp.sqrt(variance + EPSILON)


def absorb(state, queries, keyval, allowed):
    running_top, running_total, accumulated = state
    head_count = queries.shape[1]
    head_size = queries.shape[2]
    row_count = keyval.shape[0]
    width_att = head_count * head_size
    key_rows = keyval[:, :width_att].reshape(row_count, head_count, head_size)
    val_rows = keyval[:, width_att:].reshape(row_count, head_count, head_size)
    scores = (
        jnp.einsum("qhd,khd->hqk", queries, key_rows, preferred_element_type=jnp.float32)
        * SCORE_SCALE
    )
    scores = jnp.where(allowed[None], scores, NEGATIVE)
    new_top = jnp.maximum(running_top, jnp.max(scores, axis=-1))
    factor = jnp.exp(running_top - new_top)
    weights = jnp.where(allowed[None], jnp.exp(scores - new_top[:, :, None]), 0.0)
    running_total = running_total * factor + jnp.sum(weights, axis=-1)
    weights_low = weights.astype(jnp.bfloat16)
    update = jnp.einsum("hqk,khd->qhd", weights_low, val_rows, preferred_element_type=jnp.float32)
    accumulated = accumulated * jnp.transpose(factor)[:, :, None] + update
    return (new_top, running_total, accumulated)


def per_device(
    suffix_x,
    suffix_query,
    suffix_keyval,
    prefix_keyval,
    prefix_hidden,
    kv_weight,
    out_weight,
    fc_weight,
    proj_weight,
    lengths,
    placement,
    owners,
    recompute,
):
    device_count = lax.axis_size("dev")
    my_device = lax.axis_index("dev")
    slots = suffix_x.shape[1]
    block_rows = prefix_keyval.shape[1]
    width_att = suffix_query.shape[2]
    head_count = width_att // HEAD_DIM
    device_ids = jnp.arange(device_count, dtype=jnp.int32)
    hits = placement[0][:, None] == device_ids[None, :]
    device_length = jnp.sum(jnp.where(hits, lengths[0][:, None], 0), axis=0)
    my_length = jnp.sum(jnp.where(device_ids == my_device, device_length, 0))
    block_ids = jnp.arange(owners.shape[1], dtype=jnp.int32)
    chosen = recompute[0]
    chosen_owner = jnp.sum(
        jnp.where(chosen[:, None] == block_ids[None, :], owners[0][None, :], 0), axis=1
    )
    stale_device = jnp.any(chosen_owner[:, None] == device_ids[None, :], axis=0)
    queries = suffix_query[0].reshape(slots, head_count, HEAD_DIM)
    normed_prefix = normalize(prefix_hidden[0]).astype(jnp.bfloat16)
    fresh = jnp.dot(normed_prefix, kv_weight, preferred_element_type=jnp.float32).astype(
        jnp.bfloat16
    )
    my_stale = jnp.any(chosen_owner == my_device)
    local_kv = jnp.where(my_stale, fresh, prefix_keyval[0])
    skip_device = jnp.zeros_like(stale_device)
    gathered = lax.all_gather(local_kv, "dev", axis=0, tiled=True)
    prefix_count = gathered.shape[0]
    row_device = jnp.arange(prefix_count, dtype=jnp.int32) // block_rows
    skipped = jnp.any((row_device[:, None] == device_ids[None, :]) & skip_device[None, :], axis=1)
    state = (
        jnp.full((head_count, slots), NEGATIVE, jnp.float32),
        jnp.zeros((head_count, slots), jnp.float32),
        jnp.zeros((slots, head_count, HEAD_DIM), jnp.float32),
    )
    key_block = 512 if prefix_count % 512 == 0 else prefix_count
    for block_start in range(0, prefix_count, key_block):
        kept = jnp.logical_not(skipped[block_start : block_start + key_block])
        allowed = jnp.broadcast_to(kept[None, :], (slots, key_block))
        state = absorb(state, queries, gathered[block_start : block_start + key_block], allowed)
    positions = jnp.arange(slots, dtype=jnp.int32)
    causal = (positions[None, :] <= positions[:, None]) & (positions[None, :] < my_length)
    state = absorb(state, queries, suffix_keyval[0], causal)
    final_top, final_total, accumulated = state
    attended = (
        (accumulated / jnp.transpose(final_total)[:, :, None])
        .reshape(slots, width_att)
        .astype(jnp.bfloat16)
    )
    projected = jnp.dot(attended, out_weight, preferred_element_type=jnp.float32)
    residual = suffix_x[0].astype(jnp.float32) + projected
    normed = normalize(residual).astype(jnp.bfloat16)
    group_count = lax.axis_size("group")
    hidden_part = fc_weight.shape[1]
    both = jnp.concatenate([fc_weight.T, proj_weight], axis=0)
    both_half = lax.all_gather(both, "dev", axis=0)
    fc_rows = both_half[:, :hidden_part].reshape(-1, both.shape[1])
    proj_rows = both_half[:, hidden_part:].reshape(-1, both.shape[1])

    def feed(rows_in):
        inner = lax.dot_general(
            rows_in, fc_rows, (((1,), (1,)), ((), ())), preferred_element_type=jnp.float32
        )
        activated = jax.nn.gelu(inner, approximate=True).astype(jnp.bfloat16)
        return jnp.dot(activated, proj_rows, preferred_element_type=jnp.float32)

    returned = []
    for shift in range(1, group_count):
        there = [(g, (g + shift) % group_count) for g in range(group_count)]
        back = [(g, (g - shift) % group_count) for g in range(group_count)]
        partner_normed = lax.ppermute(normed, "group", there)
        partner_feed = feed(partner_normed).astype(jnp.bfloat16)
        returned.append(lax.ppermute(partner_feed, "group", back))
    feed_out = lax.optimization_barrier(feed(normed))
    for part in returned:
        feed_out = feed_out + part.astype(jnp.float32)
    live = positions[:, None] < my_length
    return jnp.where(live, residual + feed_out, 0.0).astype(jnp.bfloat16)[None]


def solution(mesh):
    return jax.shard_map(
        per_device,
        mesh=mesh,
        in_specs=(
            P("group", "dev", None),
            P("group", "dev", None),
            P("group", "dev", None),
            P("group", "dev", None),
            P("group", "dev", None),
            P(),
            P(),
            P(None, ("group", "dev")),
            P(("group", "dev"), None),
            P("group", None),
            P("group", None),
            P("group", None),
            P("group", None),
        ),
        out_specs=P("group", "dev", None),
        check_vma=False,
    )
```

```python
import jax
import jax.numpy as jnp
from jax import lax
from jax.sharding import PartitionSpec as P

HEAD_DIM = 64


NEGATIVE = -1e30
EPSILON = 1e-05
SCORE_SCALE = 0.125


def normalize(values_in):
    values_in = values_in.astype(jnp.float32)
    average = jnp.mean(values_in, axis=-1, keepdims=True)
    centered = values_in - average
    variance = jnp.mean(centered * centered, axis=-1, keepdims=True)
    return centered / jnp.sqrt(variance + EPSILON)


def absorb(state, queries, keyval, allowed):
    running_top, running_total, accumulated = state
    head_count = queries.shape[1]
    head_size = queries.shape[2]
    row_count = keyval.shape[0]
    width_att = head_count * head_size
    key_rows = keyval[:, :width_att].reshape(row_count, head_count, head_size)
    val_rows = keyval[:, width_att:].reshape(row_count, head_count, head_size)
    scores = (
        jnp.einsum("qhd,khd->hqk", queries, key_rows, preferred_element_type=jnp.float32)
        * SCORE_SCALE
    )
    scores = jnp.where(allowed[None], scores, NEGATIVE)
    new_top = jnp.maximum(running_top, jnp.max(scores, axis=-1))
    factor = jnp.exp(running_top - new_top)
    weights = jnp.where(allowed[None], jnp.exp(scores - new_top[:, :, None]), 0.0)
    running_total = running_total * factor + jnp.sum(weights, axis=-1)
    weights_low = weights.astype(jnp.bfloat16)
    update = jnp.einsum("hqk,khd->qhd", weights_low, val_rows, preferred_element_type=jnp.float32)
    accumulated = accumulated * jnp.transpose(factor)[:, :, None] + update
    return (new_top, running_total, accumulated)


def per_device(
    suffix_x,
    suffix_query,
    suffix_keyval,
    prefix_keyval,
    prefix_hidden,
    kv_weight,
    out_weight,
    fc_weight,
    proj_weight,
    lengths,
    placement,
    owners,
    recompute,
):
    device_count = lax.axis_size("dev")
    my_device = lax.axis_index("dev")
    slots = suffix_x.shape[1]
    block_rows = prefix_keyval.shape[1]
    width_att = suffix_query.shape[2]
    head_count = width_att // HEAD_DIM
    device_ids = jnp.arange(device_count, dtype=jnp.int32)
    hits = placement[0][:, None] == device_ids[None, :]
    device_length = jnp.sum(jnp.where(hits, lengths[0][:, None], 0), axis=0)
    my_length = jnp.sum(jnp.where(device_ids == my_device, device_length, 0))
    block_ids = jnp.arange(owners.shape[1], dtype=jnp.int32)
    chosen = recompute[0]
    chosen_owner = jnp.sum(
        jnp.where(chosen[:, None] == block_ids[None, :], owners[0][None, :], 0), axis=1
    )
    stale_device = jnp.any(chosen_owner[:, None] == device_ids[None, :], axis=0)
    queries = suffix_query[0].reshape(slots, head_count, HEAD_DIM)
    normed_prefix = normalize(prefix_hidden[0]).astype(jnp.bfloat16)
    fresh = jnp.dot(normed_prefix, kv_weight, preferred_element_type=jnp.float32).astype(
        jnp.bfloat16
    )
    my_stale = jnp.any(chosen_owner == my_device)
    local_kv = jnp.where(my_stale, fresh, prefix_keyval[0])
    skip_device = jnp.zeros_like(stale_device)
    gathered = lax.all_gather(local_kv, "dev", axis=0, tiled=True)
    prefix_count = gathered.shape[0]
    row_device = jnp.arange(prefix_count, dtype=jnp.int32) // block_rows
    skipped = jnp.any((row_device[:, None] == device_ids[None, :]) & skip_device[None, :], axis=1)
    state = (
        jnp.full((head_count, slots), NEGATIVE, jnp.float32),
        jnp.zeros((head_count, slots), jnp.float32),
        jnp.zeros((slots, head_count, HEAD_DIM), jnp.float32),
    )
    key_block = 512 if prefix_count % 512 == 0 else prefix_count
    for block_start in range(0, prefix_count, key_block):
        kept = jnp.logical_not(skipped[block_start : block_start + key_block])
        allowed = jnp.broadcast_to(kept[None, :], (slots, key_block))
        state = absorb(state, queries, gathered[block_start : block_start + key_block], allowed)
    positions = jnp.arange(slots, dtype=jnp.int32)
    causal = (positions[None, :] <= positions[:, None]) & (positions[None, :] < my_length)
    state = absorb(state, queries, suffix_keyval[0], causal)
    final_top, final_total, accumulated = state
    attended = (
        (accumulated / jnp.transpose(final_total)[:, :, None])
        .reshape(slots, width_att)
        .astype(jnp.bfloat16)
    )
    projected = jnp.dot(attended, out_weight, preferred_element_type=jnp.float32)
    residual = suffix_x[0].astype(jnp.float32) + projected
    normed = normalize(residual).astype(jnp.bfloat16)
    group_count = lax.axis_size("group")
    hidden_part = fc_weight.shape[1]
    both = jnp.stack([fc_weight.T, proj_weight])
    both_half = lax.all_gather(both, "dev", axis=1)
    fc_rows = both_half[0].reshape(-1, both.shape[2])
    proj_rows = both_half[1].reshape(-1, both.shape[2])

    def feed(rows_in):
        inner = lax.dot_general(
            rows_in, fc_rows, (((1,), (1,)), ((), ())), preferred_element_type=jnp.float32
        )
        activated = jax.nn.gelu(inner, approximate=True).astype(jnp.bfloat16)
        return jnp.dot(activated, proj_rows, preferred_element_type=jnp.float32)

    returned = []
    for shift in range(1, group_count):
        there = [(g, (g + shift) % group_count) for g in range(group_count)]
        back = [(g, (g - shift) % group_count) for g in range(group_count)]
        partner_normed = lax.ppermute(normed, "group", there)
        partner_feed = feed(partner_normed).astype(jnp.bfloat16)
        returned.append(lax.ppermute(partner_feed, "group", back))
    feed_out = lax.optimization_barrier(feed(normed))
    for part in returned:
        feed_out = feed_out + part.astype(jnp.float32)
    live = positions[:, None] < my_length
    return jnp.where(live, residual + feed_out, 0.0).astype(jnp.bfloat16)[None]


def solution(mesh):
    return jax.shard_map(
        per_device,
        mesh=mesh,
        in_specs=(
            P("group", "dev", None),
            P("group", "dev", None),
            P("group", "dev", None),
            P("group", "dev", None),
            P("group", "dev", None),
            P(),
            P(),
            P(None, ("group", "dev")),
            P(("group", "dev"), None),
            P("group", None),
            P("group", None),
            P("group", None),
            P("group", None),
        ),
        out_specs=P("group", "dev", None),
        check_vma=False,
    )
```

```python
import jax
import jax.numpy as jnp
from jax import lax
from jax.sharding import PartitionSpec as P

HEAD_DIM = 64


NEGATIVE = -1e30
EPSILON = 1e-05
SCORE_SCALE = 0.125


def normalize(values_in):
    values_in = values_in.astype(jnp.float32)
    average = jnp.mean(values_in, axis=-1, keepdims=True)
    centered = values_in - average
    variance = jnp.mean(centered * centered, axis=-1, keepdims=True)
    return centered / jnp.sqrt(variance + EPSILON)


def absorb(state, queries, keyval, allowed):
    running_top, running_total, accumulated = state
    head_count = queries.shape[1]
    head_size = queries.shape[2]
    row_count = keyval.shape[0]
    width_att = head_count * head_size
    key_rows = keyval[:, :width_att].reshape(row_count, head_count, head_size)
    val_rows = keyval[:, width_att:].reshape(row_count, head_count, head_size)
    scores = (
        jnp.einsum("qhd,khd->hqk", queries, key_rows, preferred_element_type=jnp.float32)
        * SCORE_SCALE
    )
    scores = jnp.where(allowed[None], scores, NEGATIVE)
    new_top = jnp.maximum(running_top, jnp.max(scores, axis=-1))
    factor = jnp.exp(running_top - new_top)
    weights = jnp.where(allowed[None], jnp.exp(scores - new_top[:, :, None]), 0.0)
    running_total = running_total * factor + jnp.sum(weights, axis=-1)
    weights_low = weights.astype(jnp.bfloat16)
    update = jnp.einsum("hqk,khd->qhd", weights_low, val_rows, preferred_element_type=jnp.float32)
    accumulated = accumulated * jnp.transpose(factor)[:, :, None] + update
    return (new_top, running_total, accumulated)


def per_device(
    suffix_x,
    suffix_query,
    suffix_keyval,
    prefix_keyval,
    prefix_hidden,
    kv_weight,
    out_weight,
    fc_weight,
    proj_weight,
    lengths,
    placement,
    owners,
    recompute,
):
    device_count = lax.axis_size("dev")
    my_device = lax.axis_index("dev")
    slots = suffix_x.shape[1]
    block_rows = prefix_keyval.shape[1]
    width_att = suffix_query.shape[2]
    head_count = width_att // HEAD_DIM
    device_ids = jnp.arange(device_count, dtype=jnp.int32)
    hits = placement[0][:, None] == device_ids[None, :]
    device_length = jnp.sum(jnp.where(hits, lengths[0][:, None], 0), axis=0)
    my_length = jnp.sum(jnp.where(device_ids == my_device, device_length, 0))
    block_ids = jnp.arange(owners.shape[1], dtype=jnp.int32)
    chosen = recompute[0]
    chosen_owner = jnp.sum(
        jnp.where(chosen[:, None] == block_ids[None, :], owners[0][None, :], 0), axis=1
    )
    stale_device = jnp.any(chosen_owner[:, None] == device_ids[None, :], axis=0)
    queries = suffix_query[0].reshape(slots, head_count, HEAD_DIM)
    normed_prefix = normalize(prefix_hidden[0]).astype(jnp.bfloat16)
    fresh = jnp.dot(normed_prefix, kv_weight, preferred_element_type=jnp.float32).astype(
        jnp.bfloat16
    )
    my_stale = jnp.any(chosen_owner == my_device)
    local_kv = jnp.where(my_stale, fresh, prefix_keyval[0])
    skip_device = jnp.zeros_like(stale_device)
    gathered = lax.all_gather(local_kv, "dev", axis=0, tiled=True)
    prefix_count = gathered.shape[0]
    row_device = jnp.arange(prefix_count, dtype=jnp.int32) // block_rows
    skipped = jnp.any((row_device[:, None] == device_ids[None, :]) & skip_device[None, :], axis=1)
    state = (
        jnp.full((head_count, slots), NEGATIVE, jnp.float32),
        jnp.zeros((head_count, slots), jnp.float32),
        jnp.zeros((slots, head_count, HEAD_DIM), jnp.float32),
    )
    key_block = 512 if prefix_count % 512 == 0 else prefix_count
    for block_start in range(0, prefix_count, key_block):
        kept = jnp.logical_not(skipped[block_start : block_start + key_block])
        allowed = jnp.broadcast_to(kept[None, :], (slots, key_block))
        state = absorb(state, queries, gathered[block_start : block_start + key_block], allowed)
    positions = jnp.arange(slots, dtype=jnp.int32)
    causal = (positions[None, :] <= positions[:, None]) & (positions[None, :] < my_length)
    state = absorb(state, queries, suffix_keyval[0], causal)
    final_top, final_total, accumulated = state
    attended = (
        (accumulated / jnp.transpose(final_total)[:, :, None])
        .reshape(slots, width_att)
        .astype(jnp.bfloat16)
    )
    projected = jnp.dot(attended, out_weight, preferred_element_type=jnp.float32)
    residual = suffix_x[0].astype(jnp.float32) + projected
    normed = normalize(residual).astype(jnp.bfloat16)
    group_count = lax.axis_size("group")
    hidden_part = fc_weight.shape[1]
    both = jnp.stack([fc_weight.T, proj_weight])
    both_half = lax.all_gather(both, "dev", axis=1)
    fc_rows = both_half[0].reshape(-1, both.shape[2])
    proj_rows = both_half[1].reshape(-1, both.shape[2])

    def feed(rows_in):
        inner = lax.dot_general(
            rows_in, fc_rows, (((1,), (1,)), ((), ())), preferred_element_type=jnp.float32
        )
        activated = jax.nn.gelu(inner, approximate=True).astype(jnp.bfloat16)
        return jnp.dot(activated, proj_rows, preferred_element_type=jnp.float32)

    chunk = slots // 2 if slots % 32 == 0 else slots
    returned = []
    for shift in range(1, group_count):
        there = [(g, (g + shift) % group_count) for g in range(group_count)]
        back = [(g, (g - shift) % group_count) for g in range(group_count)]
        partner_normed = lax.ppermute(normed, "group", there)
        pieces = []
        for start in range(0, slots, chunk):
            piece = feed(partner_normed[start : start + chunk]).astype(jnp.bfloat16)
            pieces.append(lax.ppermute(piece, "group", back))
        returned.append(jnp.concatenate(pieces, axis=0))
    feed_out = lax.optimization_barrier(feed(normed))
    for part in returned:
        feed_out = feed_out + part.astype(jnp.float32)
    live = positions[:, None] < my_length
    return jnp.where(live, residual + feed_out, 0.0).astype(jnp.bfloat16)[None]


def solution(mesh):
    return jax.shard_map(
        per_device,
        mesh=mesh,
        in_specs=(
            P("group", "dev", None),
            P("group", "dev", None),
            P("group", "dev", None),
            P("group", "dev", None),
            P("group", "dev", None),
            P(),
            P(),
            P(None, ("group", "dev")),
            P(("group", "dev"), None),
            P("group", None),
            P("group", None),
            P("group", None),
            P("group", None),
        ),
        out_specs=P("group", "dev", None),
        check_vma=False,
    )
```

```python
import jax
import jax.numpy as jnp
from jax import lax
from jax.sharding import PartitionSpec as P

HEAD_DIM = 64


NEGATIVE = -1e30
EPSILON = 1e-05
SCORE_SCALE = 0.125


def normalize(values_in):
    values_in = values_in.astype(jnp.float32)
    average = jnp.mean(values_in, axis=-1, keepdims=True)
    centered = values_in - average
    variance = jnp.mean(centered * centered, axis=-1, keepdims=True)
    return centered / jnp.sqrt(variance + EPSILON)


def absorb(state, queries, keyval, allowed):
    running_top, running_total, accumulated = state
    head_count = queries.shape[1]
    head_size = queries.shape[2]
    row_count = keyval.shape[0]
    width_att = head_count * head_size
    key_rows = keyval[:, :width_att].reshape(row_count, head_count, head_size)
    val_rows = keyval[:, width_att:].reshape(row_count, head_count, head_size)
    scores = (
        jnp.einsum("qhd,khd->hqk", queries, key_rows, preferred_element_type=jnp.float32)
        * SCORE_SCALE
    )
    scores = jnp.where(allowed[None], scores, NEGATIVE)
    new_top = jnp.maximum(running_top, jnp.max(scores, axis=-1))
    factor = jnp.exp(running_top - new_top)
    weights = jnp.where(allowed[None], jnp.exp(scores - new_top[:, :, None]), 0.0)
    running_total = running_total * factor + jnp.sum(weights, axis=-1)
    weights_low = weights.astype(jnp.bfloat16)
    update = jnp.einsum("hqk,khd->qhd", weights_low, val_rows, preferred_element_type=jnp.float32)
    accumulated = accumulated * jnp.transpose(factor)[:, :, None] + update
    return (new_top, running_total, accumulated)


def per_device(
    suffix_x,
    suffix_query,
    suffix_keyval,
    prefix_keyval,
    prefix_hidden,
    kv_weight,
    out_weight,
    fc_weight,
    proj_weight,
    lengths,
    placement,
    owners,
    recompute,
):
    device_count = lax.axis_size("dev")
    my_device = lax.axis_index("dev")
    slots = suffix_x.shape[1]
    block_rows = prefix_keyval.shape[1]
    width_att = suffix_query.shape[2]
    head_count = width_att // HEAD_DIM
    device_ids = jnp.arange(device_count, dtype=jnp.int32)
    hits = placement[0][:, None] == device_ids[None, :]
    device_length = jnp.sum(jnp.where(hits, lengths[0][:, None], 0), axis=0)
    my_length = jnp.sum(jnp.where(device_ids == my_device, device_length, 0))
    block_ids = jnp.arange(owners.shape[1], dtype=jnp.int32)
    chosen = recompute[0]
    chosen_owner = jnp.sum(
        jnp.where(chosen[:, None] == block_ids[None, :], owners[0][None, :], 0), axis=1
    )
    stale_device = jnp.any(chosen_owner[:, None] == device_ids[None, :], axis=0)
    queries = suffix_query[0].reshape(slots, head_count, HEAD_DIM)
    normed_prefix = normalize(prefix_hidden[0]).astype(jnp.bfloat16)
    fresh = jnp.dot(normed_prefix, kv_weight, preferred_element_type=jnp.float32).astype(
        jnp.bfloat16
    )
    my_stale = jnp.any(chosen_owner == my_device)
    local_kv = jnp.where(my_stale, fresh, prefix_keyval[0])
    skip_device = jnp.zeros_like(stale_device)
    gathered = lax.all_gather(local_kv, "dev", axis=0, tiled=True)
    prefix_count = gathered.shape[0]
    row_device = jnp.arange(prefix_count, dtype=jnp.int32) // block_rows
    skipped = jnp.any((row_device[:, None] == device_ids[None, :]) & skip_device[None, :], axis=1)
    state = (
        jnp.full((head_count, slots), NEGATIVE, jnp.float32),
        jnp.zeros((head_count, slots), jnp.float32),
        jnp.zeros((slots, head_count, HEAD_DIM), jnp.float32),
    )
    key_block = 512 if prefix_count % 512 == 0 else prefix_count
    for block_start in range(0, prefix_count, key_block):
        kept = jnp.logical_not(skipped[block_start : block_start + key_block])
        allowed = jnp.broadcast_to(kept[None, :], (slots, key_block))
        state = absorb(state, queries, gathered[block_start : block_start + key_block], allowed)
    positions = jnp.arange(slots, dtype=jnp.int32)
    causal = (positions[None, :] <= positions[:, None]) & (positions[None, :] < my_length)
    state = absorb(state, queries, suffix_keyval[0], causal)
    final_top, final_total, accumulated = state
    attended = (
        (accumulated / jnp.transpose(final_total)[:, :, None])
        .reshape(slots, width_att)
        .astype(jnp.bfloat16)
    )
    projected = jnp.dot(attended, out_weight, preferred_element_type=jnp.float32)
    residual = suffix_x[0].astype(jnp.float32) + projected
    normed = normalize(residual).astype(jnp.bfloat16)
    group_count = lax.axis_size("group")
    hidden_part = fc_weight.shape[1]
    both = jnp.stack([fc_weight.T, proj_weight])
    both_half = lax.all_gather(both, "dev", axis=1)
    fc_rows = both_half[0].reshape(-1, both.shape[2])
    proj_rows = both_half[1].reshape(-1, both.shape[2])

    def feed(rows_in):
        inner = lax.dot_general(
            rows_in, fc_rows, (((1,), (1,)), ((), ())), preferred_element_type=jnp.float32
        )
        activated = jax.nn.gelu(inner, approximate=True).astype(jnp.bfloat16)
        return jnp.dot(activated, proj_rows, preferred_element_type=jnp.float32)

    returned = []
    for shift in range(1, group_count):
        there = [(g, (g + shift) % group_count) for g in range(group_count)]
        back = [(g, (g - shift) % group_count) for g in range(group_count)]
        partner_normed = lax.ppermute(normed, "group", there)
        partner_feed = feed(partner_normed).astype(jnp.bfloat16)
        returned.append(lax.ppermute(partner_feed, "group", back))
    summed = lax.optimization_barrier(residual + feed(normed))
    for part in returned:
        summed = summed + part.astype(jnp.float32)
    live = positions[:, None] < my_length
    return jnp.where(live, summed, 0.0).astype(jnp.bfloat16)[None]


def solution(mesh):
    return jax.shard_map(
        per_device,
        mesh=mesh,
        in_specs=(
            P("group", "dev", None),
            P("group", "dev", None),
            P("group", "dev", None),
            P("group", "dev", None),
            P("group", "dev", None),
            P(),
            P(),
            P(None, ("group", "dev")),
            P(("group", "dev"), None),
            P("group", None),
            P("group", None),
            P("group", None),
            P("group", None),
        ),
        out_specs=P("group", "dev", None),
        check_vma=False,
    )
```

```python
import functools

import jax
import jax.numpy as jnp
from jax import lax
from jax.sharding import PartitionSpec as P

HEAD_DIM = 64


NEGATIVE = -1e30
EPSILON = 1e-05
SCORE_SCALE = 0.125


def normalize(values_in):
    values_in = values_in.astype(jnp.float32)
    average = jnp.mean(values_in, axis=-1, keepdims=True)
    centered = values_in - average
    variance = jnp.mean(centered * centered, axis=-1, keepdims=True)
    return centered / jnp.sqrt(variance + EPSILON)


def absorb(state, queries, keyval, allowed):
    running_top, running_total, accumulated = state
    head_count = queries.shape[1]
    head_size = queries.shape[2]
    row_count = keyval.shape[0]
    width_att = head_count * head_size
    key_rows = keyval[:, :width_att].reshape(row_count, head_count, head_size)
    val_rows = keyval[:, width_att:].reshape(row_count, head_count, head_size)
    scores = (
        jnp.einsum("qhd,khd->hqk", queries, key_rows, preferred_element_type=jnp.float32)
        * SCORE_SCALE
    )
    scores = jnp.where(allowed[None], scores, NEGATIVE)
    new_top = jnp.maximum(running_top, jnp.max(scores, axis=-1))
    factor = jnp.exp(running_top - new_top)
    weights = jnp.where(allowed[None], jnp.exp(scores - new_top[:, :, None]), 0.0)
    running_total = running_total * factor + jnp.sum(weights, axis=-1)
    weights_low = weights.astype(jnp.bfloat16)
    update = jnp.einsum("hqk,khd->qhd", weights_low, val_rows, preferred_element_type=jnp.float32)
    accumulated = accumulated * jnp.transpose(factor)[:, :, None] + update
    return (new_top, running_total, accumulated)


def ring_gather(shard, forward, backward, swap, steps_forward, steps_backward):
    pieces = [shard]
    ahead = shard
    behind = shard
    for step in range(steps_forward):
        ahead = lax.ppermute(ahead, "dev", forward)
        pieces.append(ahead)
        if step < steps_backward:
            behind = lax.ppermute(behind, "dev", backward)
            pieces.append(behind)
    pieces = pieces + [lax.ppermute(piece, "dev", swap) for piece in pieces]
    return jnp.concatenate(pieces, axis=1)


def plan_ring(mesh):
    devices = mesh.devices
    device_count = devices.shape[1]
    if device_count % 2 or device_count < 4:
        return None
    chip_count = device_count // 2
    try:
        grids = []
        for row in devices:
            coords = [tuple(row[2 * k].coords) for k in range(chip_count)]
            if any(tuple(row[2 * k + 1].coords) != coords[k] for k in range(chip_count)):
                return None
            grids.append(coords)
    except AttributeError:
        return None
    coords = grids[0]
    varying = [axis for axis in range(len(coords[0])) if len({c[axis] for c in coords}) > 1]
    if len(varying) != 2:
        return None
    long_axis, short_axis = varying
    if len({c[short_axis] for c in coords}) != 2:
        long_axis, short_axis = short_axis, long_axis
    if len({c[short_axis] for c in coords}) != 2:
        return None
    low, high = sorted({c[short_axis] for c in coords})
    along = sorted({c[long_axis] for c in coords})
    place = {(c[short_axis], c[long_axis]): k for k, c in enumerate(coords)}
    if len(place) != chip_count:
        return None
    cycle = [place[(low, a)] for a in along] + [place[(high, a)] for a in reversed(along)]
    for coords_g in grids:
        for i in range(chip_count):
            first = coords_g[cycle[i]]
            second = coords_g[cycle[(i + 1) % chip_count]]
            if sum(abs(p - q) for p, q in zip(first, second)) != 1:
                return None
    after = {cycle[i]: cycle[(i + 1) % chip_count] for i in range(chip_count)}
    before = {cycle[i]: cycle[(i - 1) % chip_count] for i in range(chip_count)}
    forward = [(2 * k + c, 2 * after[k] + c) for k in range(chip_count) for c in range(2)]
    backward = [(2 * k + c, 2 * before[k] + c) for k in range(chip_count) for c in range(2)]
    swap = [(2 * k + c, 2 * k + 1 - c) for k in range(chip_count) for c in range(2)]
    steps_forward = chip_count // 2
    return forward, backward, swap, steps_forward, chip_count - 1 - steps_forward


def per_device(
    ring_plan,
    suffix_x,
    suffix_query,
    suffix_keyval,
    prefix_keyval,
    prefix_hidden,
    kv_weight,
    out_weight,
    fc_weight,
    proj_weight,
    lengths,
    placement,
    owners,
    recompute,
):
    device_count = lax.axis_size("dev")
    my_device = lax.axis_index("dev")
    slots = suffix_x.shape[1]
    block_rows = prefix_keyval.shape[1]
    width_att = suffix_query.shape[2]
    head_count = width_att // HEAD_DIM
    device_ids = jnp.arange(device_count, dtype=jnp.int32)
    hits = placement[0][:, None] == device_ids[None, :]
    device_length = jnp.sum(jnp.where(hits, lengths[0][:, None], 0), axis=0)
    my_length = jnp.sum(jnp.where(device_ids == my_device, device_length, 0))
    block_ids = jnp.arange(owners.shape[1], dtype=jnp.int32)
    chosen = recompute[0]
    chosen_owner = jnp.sum(
        jnp.where(chosen[:, None] == block_ids[None, :], owners[0][None, :], 0), axis=1
    )
    stale_device = jnp.any(chosen_owner[:, None] == device_ids[None, :], axis=0)
    queries = suffix_query[0].reshape(slots, head_count, HEAD_DIM)
    normed_prefix = normalize(prefix_hidden[0]).astype(jnp.bfloat16)
    fresh = jnp.dot(normed_prefix, kv_weight, preferred_element_type=jnp.float32).astype(
        jnp.bfloat16
    )
    my_stale = jnp.any(chosen_owner == my_device)
    local_kv = jnp.where(my_stale, fresh, prefix_keyval[0])
    skip_device = jnp.zeros_like(stale_device)
    gathered = lax.all_gather(local_kv, "dev", axis=0, tiled=True)
    prefix_count = gathered.shape[0]
    row_device = jnp.arange(prefix_count, dtype=jnp.int32) // block_rows
    skipped = jnp.any((row_device[:, None] == device_ids[None, :]) & skip_device[None, :], axis=1)
    state = (
        jnp.full((head_count, slots), NEGATIVE, jnp.float32),
        jnp.zeros((head_count, slots), jnp.float32),
        jnp.zeros((slots, head_count, HEAD_DIM), jnp.float32),
    )
    key_block = 512 if prefix_count % 512 == 0 else prefix_count
    for block_start in range(0, prefix_count, key_block):
        kept = jnp.logical_not(skipped[block_start : block_start + key_block])
        allowed = jnp.broadcast_to(kept[None, :], (slots, key_block))
        state = absorb(state, queries, gathered[block_start : block_start + key_block], allowed)
    positions = jnp.arange(slots, dtype=jnp.int32)
    causal = (positions[None, :] <= positions[:, None]) & (positions[None, :] < my_length)
    state = absorb(state, queries, suffix_keyval[0], causal)
    final_top, final_total, accumulated = state
    attended = (
        (accumulated / jnp.transpose(final_total)[:, :, None])
        .reshape(slots, width_att)
        .astype(jnp.bfloat16)
    )
    projected = jnp.dot(attended, out_weight, preferred_element_type=jnp.float32)
    residual = suffix_x[0].astype(jnp.float32) + projected
    normed = normalize(residual).astype(jnp.bfloat16)
    group_count = lax.axis_size("group")
    hidden_part = fc_weight.shape[1]
    both = jnp.stack([fc_weight.T, proj_weight])
    if ring_plan is None:
        both_half = lax.all_gather(both, "dev", axis=1)
    else:
        both_half = ring_gather(both, *ring_plan)
    fc_rows = both_half[0].reshape(-1, both.shape[2])
    proj_rows = both_half[1].reshape(-1, both.shape[2])

    def feed(rows_in):
        inner = lax.dot_general(
            rows_in, fc_rows, (((1,), (1,)), ((), ())), preferred_element_type=jnp.float32
        )
        activated = jax.nn.gelu(inner, approximate=True).astype(jnp.bfloat16)
        return jnp.dot(activated, proj_rows, preferred_element_type=jnp.float32)

    returned = []
    for shift in range(1, group_count):
        there = [(g, (g + shift) % group_count) for g in range(group_count)]
        back = [(g, (g - shift) % group_count) for g in range(group_count)]
        partner_normed = lax.ppermute(normed, "group", there)
        partner_feed = feed(partner_normed).astype(jnp.bfloat16)
        returned.append(lax.ppermute(partner_feed, "group", back))
    summed = lax.optimization_barrier(residual + feed(normed))
    for part in returned:
        summed = summed + part.astype(jnp.float32)
    live = positions[:, None] < my_length
    return jnp.where(live, summed, 0.0).astype(jnp.bfloat16)[None]


def solution(mesh):
    return jax.shard_map(
        functools.partial(per_device, plan_ring(mesh)),
        mesh=mesh,
        in_specs=(
            P("group", "dev", None),
            P("group", "dev", None),
            P("group", "dev", None),
            P("group", "dev", None),
            P("group", "dev", None),
            P(),
            P(),
            P(None, ("group", "dev")),
            P(("group", "dev"), None),
            P("group", None),
            P("group", None),
            P("group", None),
            P("group", None),
        ),
        out_specs=P("group", "dev", None),
        check_vma=False,
    )
```

```python
import functools

import jax
import jax.numpy as jnp
from jax import lax
from jax.sharding import PartitionSpec as P

HEAD_DIM = 64


NEGATIVE = -1e30
EPSILON = 1e-05
SCORE_SCALE = 0.125


def normalize(values_in):
    values_in = values_in.astype(jnp.float32)
    average = jnp.mean(values_in, axis=-1, keepdims=True)
    centered = values_in - average
    variance = jnp.mean(centered * centered, axis=-1, keepdims=True)
    return centered / jnp.sqrt(variance + EPSILON)


def absorb(state, queries, keyval, allowed):
    running_top, running_total, accumulated = state
    head_count = queries.shape[1]
    head_size = queries.shape[2]
    row_count = keyval.shape[0]
    width_att = head_count * head_size
    key_rows = keyval[:, :width_att].reshape(row_count, head_count, head_size)
    val_rows = keyval[:, width_att:].reshape(row_count, head_count, head_size)
    scores = (
        jnp.einsum("qhd,khd->hqk", queries, key_rows, preferred_element_type=jnp.float32)
        * SCORE_SCALE
    )
    scores = jnp.where(allowed[None], scores, NEGATIVE)
    new_top = jnp.maximum(running_top, jnp.max(scores, axis=-1))
    factor = jnp.exp(running_top - new_top)
    weights = jnp.where(allowed[None], jnp.exp(scores - new_top[:, :, None]), 0.0)
    running_total = running_total * factor + jnp.sum(weights, axis=-1)
    weights_low = weights.astype(jnp.bfloat16)
    update = jnp.einsum("hqk,khd->qhd", weights_low, val_rows, preferred_element_type=jnp.float32)
    accumulated = accumulated * jnp.transpose(factor)[:, :, None] + update
    return (new_top, running_total, accumulated)


def ring_first(shard, forward, backward, swap, steps_forward, steps_backward):
    ahead = lax.ppermute(shard, "dev", forward)
    behind = lax.ppermute(shard, "dev", backward) if steps_backward else shard
    return ahead, behind


def ring_rest(shard, ahead, behind, forward, backward, swap, steps_forward, steps_backward):
    pieces = [shard, ahead] + ([behind] if steps_backward else [])
    for step in range(1, steps_forward):
        ahead = lax.ppermute(ahead, "dev", forward)
        pieces.append(ahead)
        if step < steps_backward:
            behind = lax.ppermute(behind, "dev", backward)
            pieces.append(behind)
    pieces = pieces + [lax.ppermute(piece, "dev", swap) for piece in pieces]
    return jnp.concatenate(pieces, axis=1)


def plan_ring(mesh):
    devices = mesh.devices
    device_count = devices.shape[1]
    if device_count % 2 or device_count < 4:
        return None
    chip_count = device_count // 2
    try:
        grids = []
        for row in devices:
            coords = [tuple(row[2 * k].coords) for k in range(chip_count)]
            if any(tuple(row[2 * k + 1].coords) != coords[k] for k in range(chip_count)):
                return None
            grids.append(coords)
    except AttributeError:
        return None
    coords = grids[0]
    varying = [axis for axis in range(len(coords[0])) if len({c[axis] for c in coords}) > 1]
    if len(varying) != 2:
        return None
    long_axis, short_axis = varying
    if len({c[short_axis] for c in coords}) != 2:
        long_axis, short_axis = short_axis, long_axis
    if len({c[short_axis] for c in coords}) != 2:
        return None
    low, high = sorted({c[short_axis] for c in coords})
    along = sorted({c[long_axis] for c in coords})
    place = {(c[short_axis], c[long_axis]): k for k, c in enumerate(coords)}
    if len(place) != chip_count:
        return None
    cycle = [place[(low, a)] for a in along] + [place[(high, a)] for a in reversed(along)]
    for coords_g in grids:
        for i in range(chip_count):
            first = coords_g[cycle[i]]
            second = coords_g[cycle[(i + 1) % chip_count]]
            if sum(abs(p - q) for p, q in zip(first, second)) != 1:
                return None
    after = {cycle[i]: cycle[(i + 1) % chip_count] for i in range(chip_count)}
    before = {cycle[i]: cycle[(i - 1) % chip_count] for i in range(chip_count)}
    forward = [(2 * k + c, 2 * after[k] + c) for k in range(chip_count) for c in range(2)]
    backward = [(2 * k + c, 2 * before[k] + c) for k in range(chip_count) for c in range(2)]
    swap = [(2 * k + c, 2 * k + 1 - c) for k in range(chip_count) for c in range(2)]
    steps_forward = chip_count // 2
    return forward, backward, swap, steps_forward, chip_count - 1 - steps_forward


def per_device(
    ring_plan,
    suffix_x,
    suffix_query,
    suffix_keyval,
    prefix_keyval,
    prefix_hidden,
    kv_weight,
    out_weight,
    fc_weight,
    proj_weight,
    lengths,
    placement,
    owners,
    recompute,
):
    device_count = lax.axis_size("dev")
    my_device = lax.axis_index("dev")
    slots = suffix_x.shape[1]
    block_rows = prefix_keyval.shape[1]
    width_att = suffix_query.shape[2]
    head_count = width_att // HEAD_DIM
    device_ids = jnp.arange(device_count, dtype=jnp.int32)
    hits = placement[0][:, None] == device_ids[None, :]
    device_length = jnp.sum(jnp.where(hits, lengths[0][:, None], 0), axis=0)
    my_length = jnp.sum(jnp.where(device_ids == my_device, device_length, 0))
    block_ids = jnp.arange(owners.shape[1], dtype=jnp.int32)
    chosen = recompute[0]
    chosen_owner = jnp.sum(
        jnp.where(chosen[:, None] == block_ids[None, :], owners[0][None, :], 0), axis=1
    )
    stale_device = jnp.any(chosen_owner[:, None] == device_ids[None, :], axis=0)
    queries = suffix_query[0].reshape(slots, head_count, HEAD_DIM)
    normed_prefix = normalize(prefix_hidden[0]).astype(jnp.bfloat16)
    fresh = jnp.dot(normed_prefix, kv_weight, preferred_element_type=jnp.float32).astype(
        jnp.bfloat16
    )
    my_stale = jnp.any(chosen_owner == my_device)
    local_kv = jnp.where(my_stale, fresh, prefix_keyval[0])
    skip_device = jnp.zeros_like(stale_device)
    both = jnp.stack([fc_weight.T, proj_weight])
    if ring_plan is not None:
        ahead, behind = ring_first(both, *ring_plan)
    gathered = lax.all_gather(local_kv, "dev", axis=0, tiled=True)
    if ring_plan is not None:
        gathered, ahead, behind = lax.optimization_barrier((gathered, ahead, behind))
    prefix_count = gathered.shape[0]
    row_device = jnp.arange(prefix_count, dtype=jnp.int32) // block_rows
    skipped = jnp.any((row_device[:, None] == device_ids[None, :]) & skip_device[None, :], axis=1)
    state = (
        jnp.full((head_count, slots), NEGATIVE, jnp.float32),
        jnp.zeros((head_count, slots), jnp.float32),
        jnp.zeros((slots, head_count, HEAD_DIM), jnp.float32),
    )
    key_block = 512 if prefix_count % 512 == 0 else prefix_count
    for block_start in range(0, prefix_count, key_block):
        kept = jnp.logical_not(skipped[block_start : block_start + key_block])
        allowed = jnp.broadcast_to(kept[None, :], (slots, key_block))
        state = absorb(state, queries, gathered[block_start : block_start + key_block], allowed)
    positions = jnp.arange(slots, dtype=jnp.int32)
    causal = (positions[None, :] <= positions[:, None]) & (positions[None, :] < my_length)
    state = absorb(state, queries, suffix_keyval[0], causal)
    final_top, final_total, accumulated = state
    attended = (
        (accumulated / jnp.transpose(final_total)[:, :, None])
        .reshape(slots, width_att)
        .astype(jnp.bfloat16)
    )
    projected = jnp.dot(attended, out_weight, preferred_element_type=jnp.float32)
    residual = suffix_x[0].astype(jnp.float32) + projected
    normed = normalize(residual).astype(jnp.bfloat16)
    group_count = lax.axis_size("group")
    hidden_part = fc_weight.shape[1]
    if ring_plan is None:
        both_half = lax.all_gather(both, "dev", axis=1)
    else:
        both_half = ring_rest(both, ahead, behind, *ring_plan)
    fc_rows = both_half[0].reshape(-1, both.shape[2])
    proj_rows = both_half[1].reshape(-1, both.shape[2])

    def feed(rows_in):
        inner = lax.dot_general(
            rows_in, fc_rows, (((1,), (1,)), ((), ())), preferred_element_type=jnp.float32
        )
        activated = jax.nn.gelu(inner, approximate=True).astype(jnp.bfloat16)
        return jnp.dot(activated, proj_rows, preferred_element_type=jnp.float32)

    returned = []
    for shift in range(1, group_count):
        there = [(g, (g + shift) % group_count) for g in range(group_count)]
        back = [(g, (g - shift) % group_count) for g in range(group_count)]
        partner_normed = lax.ppermute(normed, "group", there)
        partner_feed = feed(partner_normed).astype(jnp.bfloat16)
        returned.append(lax.ppermute(partner_feed, "group", back))
    summed = lax.optimization_barrier(residual + feed(normed))
    for part in returned:
        summed = summed + part.astype(jnp.float32)
    live = positions[:, None] < my_length
    return jnp.where(live, summed, 0.0).astype(jnp.bfloat16)[None]


def solution(mesh):
    return jax.shard_map(
        functools.partial(per_device, plan_ring(mesh)),
        mesh=mesh,
        in_specs=(
            P("group", "dev", None),
            P("group", "dev", None),
            P("group", "dev", None),
            P("group", "dev", None),
            P("group", "dev", None),
            P(),
            P(),
            P(None, ("group", "dev")),
            P(("group", "dev"), None),
            P("group", None),
            P("group", None),
            P("group", None),
            P("group", None),
        ),
        out_specs=P("group", "dev", None),
        check_vma=False,
    )
```

```python
import functools

import jax
import jax.numpy as jnp
from jax import lax
from jax.sharding import PartitionSpec as P

HEAD_DIM = 64


NEGATIVE = -1e30
EPSILON = 1e-05
SCORE_SCALE = 0.125


def normalize(values_in):
    values_in = values_in.astype(jnp.float32)
    average = jnp.mean(values_in, axis=-1, keepdims=True)
    centered = values_in - average
    variance = jnp.mean(centered * centered, axis=-1, keepdims=True)
    return centered / jnp.sqrt(variance + EPSILON)


def absorb(state, queries, keyval, allowed):
    running_top, running_total, accumulated = state
    head_count = queries.shape[1]
    head_size = queries.shape[2]
    row_count = keyval.shape[0]
    width_att = head_count * head_size
    key_rows = keyval[:, :width_att].reshape(row_count, head_count, head_size)
    val_rows = keyval[:, width_att:].reshape(row_count, head_count, head_size)
    scores = (
        jnp.einsum("qhd,khd->hqk", queries, key_rows, preferred_element_type=jnp.float32)
        * SCORE_SCALE
    )
    scores = jnp.where(allowed[None], scores, NEGATIVE)
    new_top = jnp.maximum(running_top, jnp.max(scores, axis=-1))
    factor = jnp.exp(running_top - new_top)
    weights = jnp.where(allowed[None], jnp.exp(scores - new_top[:, :, None]), 0.0)
    running_total = running_total * factor + jnp.sum(weights, axis=-1)
    weights_low = weights.astype(jnp.bfloat16)
    update = jnp.einsum("hqk,khd->qhd", weights_low, val_rows, preferred_element_type=jnp.float32)
    accumulated = accumulated * jnp.transpose(factor)[:, :, None] + update
    return (new_top, running_total, accumulated)


def ring_issue(state, plan):
    forward, backward, full_steps, split = plan[0], plan[1], plan[3], plan[4]
    ahead, behind, pieces, done = state
    if done < full_steps:
        return lax.ppermute(ahead, "dev", forward), lax.ppermute(behind, "dev", backward)
    if done == full_steps and split:
        cut = ahead.shape[1] // 2
        return (
            lax.ppermute(ahead[:, :cut], "dev", forward),
            lax.ppermute(behind[:, cut:], "dev", backward),
        )
    return None


def ring_land(state, plan, sent, tie):
    ahead, behind, pieces, done = state
    if sent is None:
        return state, tie
    first, second = sent
    tie, first, second = lax.optimization_barrier((tie, first, second))
    if done < plan[3]:
        return (first, second, pieces + [first, second], done + 1), tie
    return (ahead, behind, pieces + [first, second], done + 1), tie


def ring_step(state, plan, tie):
    return ring_land(state, plan, ring_issue(state, plan), tie)


def ring_finish(state, plan):
    swap = plan[2]
    while state[3] <= plan[3]:
        state, _ = ring_step(state, plan, jnp.zeros((), jnp.float32))
    pieces = state[2]
    pieces = pieces + [lax.ppermute(piece, "dev", swap) for piece in pieces]
    rows = sum(piece.shape[1] for piece in pieces)
    full = jnp.zeros((pieces[0].shape[0], rows, pieces[0].shape[2]), pieces[0].dtype)
    offset = 0
    for piece in pieces:
        full = lax.dynamic_update_slice(full, piece, (0, offset, 0))
        offset += piece.shape[1]
    return full


def plan_ring(mesh):
    devices = mesh.devices
    device_count = devices.shape[1]
    if device_count % 2 or device_count < 4:
        return None
    chip_count = device_count // 2
    try:
        grids = []
        for row in devices:
            coords = [tuple(row[2 * k].coords) for k in range(chip_count)]
            if any(tuple(row[2 * k + 1].coords) != coords[k] for k in range(chip_count)):
                return None
            grids.append(coords)
    except AttributeError:
        return None
    coords = grids[0]
    varying = [axis for axis in range(len(coords[0])) if len({c[axis] for c in coords}) > 1]
    if len(varying) != 2:
        return None
    long_axis, short_axis = varying
    if len({c[short_axis] for c in coords}) != 2:
        long_axis, short_axis = short_axis, long_axis
    if len({c[short_axis] for c in coords}) != 2:
        return None
    low, high = sorted({c[short_axis] for c in coords})
    along = sorted({c[long_axis] for c in coords})
    place = {(c[short_axis], c[long_axis]): k for k, c in enumerate(coords)}
    if len(place) != chip_count:
        return None
    cycle = [place[(low, a)] for a in along] + [place[(high, a)] for a in reversed(along)]
    for coords_g in grids:
        for i in range(chip_count):
            first = coords_g[cycle[i]]
            second = coords_g[cycle[(i + 1) % chip_count]]
            if sum(abs(p - q) for p, q in zip(first, second)) != 1:
                return None
    after = {cycle[i]: cycle[(i + 1) % chip_count] for i in range(chip_count)}
    before = {cycle[i]: cycle[(i - 1) % chip_count] for i in range(chip_count)}
    forward = [(2 * k + c, 2 * after[k] + c) for k in range(chip_count) for c in range(2)]
    backward = [(2 * k + c, 2 * before[k] + c) for k in range(chip_count) for c in range(2)]
    swap = [(2 * k + c, 2 * k + 1 - c) for k in range(chip_count) for c in range(2)]
    full_steps = (chip_count - 1) // 2
    return forward, backward, swap, full_steps, chip_count % 2 == 0


def per_device(
    ring_plan,
    suffix_x,
    suffix_query,
    suffix_keyval,
    prefix_keyval,
    prefix_hidden,
    kv_weight,
    out_weight,
    fc_weight,
    proj_weight,
    lengths,
    placement,
    owners,
    recompute,
):
    device_count = lax.axis_size("dev")
    my_device = lax.axis_index("dev")
    slots = suffix_x.shape[1]
    block_rows = prefix_keyval.shape[1]
    width_att = suffix_query.shape[2]
    head_count = width_att // HEAD_DIM
    device_ids = jnp.arange(device_count, dtype=jnp.int32)
    hits = placement[0][:, None] == device_ids[None, :]
    device_length = jnp.sum(jnp.where(hits, lengths[0][:, None], 0), axis=0)
    my_length = jnp.sum(jnp.where(device_ids == my_device, device_length, 0))
    block_ids = jnp.arange(owners.shape[1], dtype=jnp.int32)
    chosen = recompute[0]
    chosen_owner = jnp.sum(
        jnp.where(chosen[:, None] == block_ids[None, :], owners[0][None, :], 0), axis=1
    )
    stale_device = jnp.any(chosen_owner[:, None] == device_ids[None, :], axis=0)
    queries = suffix_query[0].reshape(slots, head_count, HEAD_DIM)
    normed_prefix = normalize(prefix_hidden[0]).astype(jnp.bfloat16)
    fresh = jnp.dot(normed_prefix, kv_weight, preferred_element_type=jnp.float32).astype(
        jnp.bfloat16
    )
    my_stale = jnp.any(chosen_owner == my_device)
    local_kv = jnp.where(my_stale, fresh, prefix_keyval[0])
    skip_device = jnp.zeros_like(stale_device)
    both = jnp.stack([fc_weight.T, proj_weight])
    if ring_plan is not None:
        ring = (both, both, [both], 0)
        ring, local_kv = ring_step(ring, ring_plan, local_kv)
        sent = ring_issue(ring, ring_plan)
    gathered = lax.all_gather(local_kv, "dev", axis=0, tiled=True)
    if ring_plan is not None:
        ring, gathered = ring_land(ring, ring_plan, sent, gathered)
    prefix_count = gathered.shape[0]
    row_device = jnp.arange(prefix_count, dtype=jnp.int32) // block_rows
    skipped = jnp.any((row_device[:, None] == device_ids[None, :]) & skip_device[None, :], axis=1)
    state = (
        jnp.full((head_count, slots), NEGATIVE, jnp.float32),
        jnp.zeros((head_count, slots), jnp.float32),
        jnp.zeros((slots, head_count, HEAD_DIM), jnp.float32),
    )
    key_block = 512 if prefix_count % 512 == 0 else prefix_count
    for block_start in range(0, prefix_count, key_block):
        kept = jnp.logical_not(skipped[block_start : block_start + key_block])
        allowed = jnp.broadcast_to(kept[None, :], (slots, key_block))
        state = absorb(state, queries, gathered[block_start : block_start + key_block], allowed)
    positions = jnp.arange(slots, dtype=jnp.int32)
    causal = (positions[None, :] <= positions[:, None]) & (positions[None, :] < my_length)
    state = absorb(state, queries, suffix_keyval[0], causal)
    final_top, final_total, accumulated = state
    attended = (
        (accumulated / jnp.transpose(final_total)[:, :, None])
        .reshape(slots, width_att)
        .astype(jnp.bfloat16)
    )
    projected = jnp.dot(attended, out_weight, preferred_element_type=jnp.float32)
    residual = suffix_x[0].astype(jnp.float32) + projected
    normed = normalize(residual).astype(jnp.bfloat16)
    if ring_plan is not None:
        ring, normed = ring_step(ring, ring_plan, normed)
    group_count = lax.axis_size("group")
    hidden_part = fc_weight.shape[1]
    if ring_plan is None:
        both_half = lax.all_gather(both, "dev", axis=1)
    else:
        both_half = ring_finish(ring, ring_plan)
    fc_rows = both_half[0].reshape(-1, both.shape[2])
    proj_rows = both_half[1].reshape(-1, both.shape[2])

    def feed(rows_in):
        inner = lax.dot_general(
            rows_in, fc_rows, (((1,), (1,)), ((), ())), preferred_element_type=jnp.float32
        )
        activated = jax.nn.gelu(inner, approximate=True).astype(jnp.bfloat16)
        return jnp.dot(activated, proj_rows, preferred_element_type=jnp.float32)

    returned = []
    for shift in range(1, group_count):
        there = [(g, (g + shift) % group_count) for g in range(group_count)]
        back = [(g, (g - shift) % group_count) for g in range(group_count)]
        partner_normed = lax.ppermute(normed, "group", there)
        partner_feed = feed(partner_normed).astype(jnp.bfloat16)
        returned.append(lax.ppermute(partner_feed, "group", back))
    summed = lax.optimization_barrier(residual + feed(normed))
    for part in returned:
        summed = summed + part.astype(jnp.float32)
    live = positions[:, None] < my_length
    return jnp.where(live, summed, 0.0).astype(jnp.bfloat16)[None]


def solution(mesh):
    return jax.shard_map(
        functools.partial(per_device, plan_ring(mesh)),
        mesh=mesh,
        in_specs=(
            P("group", "dev", None),
            P("group", "dev", None),
            P("group", "dev", None),
            P("group", "dev", None),
            P("group", "dev", None),
            P(),
            P(),
            P(None, ("group", "dev")),
            P(("group", "dev"), None),
            P("group", None),
            P("group", None),
            P("group", None),
            P("group", None),
        ),
        out_specs=P("group", "dev", None),
        check_vma=False,
    )
```

```python
import functools

import jax
import jax.numpy as jnp
from jax import lax
from jax.sharding import PartitionSpec as P

HEAD_DIM = 64


NEGATIVE = -1e30
EPSILON = 1e-05
SCORE_SCALE = 0.125


def normalize(values_in):
    values_in = values_in.astype(jnp.float32)
    average = jnp.mean(values_in, axis=-1, keepdims=True)
    centered = values_in - average
    variance = jnp.mean(centered * centered, axis=-1, keepdims=True)
    return centered / jnp.sqrt(variance + EPSILON)


def absorb(state, queries, keyval, allowed):
    running_top, running_total, accumulated = state
    head_count = queries.shape[1]
    head_size = queries.shape[2]
    row_count = keyval.shape[0]
    width_att = head_count * head_size
    key_rows = keyval[:, :width_att].reshape(row_count, head_count, head_size)
    val_rows = keyval[:, width_att:].reshape(row_count, head_count, head_size)
    scores = (
        jnp.einsum("qhd,khd->hqk", queries, key_rows, preferred_element_type=jnp.float32)
        * SCORE_SCALE
    )
    scores = jnp.where(allowed[None], scores, NEGATIVE)
    new_top = jnp.maximum(running_top, jnp.max(scores, axis=-1))
    factor = jnp.exp(running_top - new_top)
    weights = jnp.where(allowed[None], jnp.exp(scores - new_top[:, :, None]), 0.0)
    running_total = running_total * factor + jnp.sum(weights, axis=-1)
    weights_low = weights.astype(jnp.bfloat16)
    update = jnp.einsum("hqk,khd->qhd", weights_low, val_rows, preferred_element_type=jnp.float32)
    accumulated = accumulated * jnp.transpose(factor)[:, :, None] + update
    return (new_top, running_total, accumulated)


def ring_gather(shard, forward, backward, swap, steps_forward, steps_backward):
    pieces = [shard]
    ahead = shard
    behind = shard
    for step in range(steps_forward):
        ahead = lax.ppermute(ahead, "dev", forward)
        pieces.append(ahead)
        if step < steps_backward:
            behind = lax.ppermute(behind, "dev", backward)
            pieces.append(behind)
    pieces = pieces + [lax.ppermute(piece, "dev", swap) for piece in pieces]
    return jnp.concatenate(pieces, axis=1)


def plan_ring(mesh):
    devices = mesh.devices
    device_count = devices.shape[1]
    if device_count % 2 or device_count < 4:
        return None
    chip_count = device_count // 2
    try:
        grids = []
        for row in devices:
            coords = [tuple(row[2 * k].coords) for k in range(chip_count)]
            if any(tuple(row[2 * k + 1].coords) != coords[k] for k in range(chip_count)):
                return None
            grids.append(coords)
    except AttributeError:
        return None
    coords = grids[0]
    varying = [axis for axis in range(len(coords[0])) if len({c[axis] for c in coords}) > 1]
    if len(varying) != 2:
        return None
    long_axis, short_axis = varying
    if len({c[short_axis] for c in coords}) != 2:
        long_axis, short_axis = short_axis, long_axis
    if len({c[short_axis] for c in coords}) != 2:
        return None
    low, high = sorted({c[short_axis] for c in coords})
    along = sorted({c[long_axis] for c in coords})
    place = {(c[short_axis], c[long_axis]): k for k, c in enumerate(coords)}
    if len(place) != chip_count:
        return None
    cycle = [place[(low, a)] for a in along] + [place[(high, a)] for a in reversed(along)]
    for coords_g in grids:
        for i in range(chip_count):
            first = coords_g[cycle[i]]
            second = coords_g[cycle[(i + 1) % chip_count]]
            if sum(abs(p - q) for p, q in zip(first, second)) != 1:
                return None
    after = {cycle[i]: cycle[(i + 1) % chip_count] for i in range(chip_count)}
    before = {cycle[i]: cycle[(i - 1) % chip_count] for i in range(chip_count)}
    forward = [(2 * k + c, 2 * after[k] + c) for k in range(chip_count) for c in range(2)]
    backward = [(2 * k + c, 2 * before[k] + c) for k in range(chip_count) for c in range(2)]
    swap = [(2 * k + c, 2 * k + 1 - c) for k in range(chip_count) for c in range(2)]
    steps_forward = chip_count // 2
    return forward, backward, swap, steps_forward, chip_count - 1 - steps_forward


def per_device(
    ring_plan,
    suffix_x,
    suffix_query,
    suffix_keyval,
    prefix_keyval,
    prefix_hidden,
    kv_weight,
    out_weight,
    fc_weight,
    proj_weight,
    lengths,
    placement,
    owners,
    recompute,
):
    device_count = lax.axis_size("dev")
    my_device = lax.axis_index("dev")
    slots = suffix_x.shape[1]
    block_rows = prefix_keyval.shape[1]
    width_att = suffix_query.shape[2]
    head_count = width_att // HEAD_DIM
    device_ids = jnp.arange(device_count, dtype=jnp.int32)
    hits = placement[0][:, None] == device_ids[None, :]
    device_length = jnp.sum(jnp.where(hits, lengths[0][:, None], 0), axis=0)
    my_length = jnp.sum(jnp.where(device_ids == my_device, device_length, 0))
    block_ids = jnp.arange(owners.shape[1], dtype=jnp.int32)
    chosen = recompute[0]
    chosen_owner = jnp.sum(
        jnp.where(chosen[:, None] == block_ids[None, :], owners[0][None, :], 0), axis=1
    )
    stale_device = jnp.any(chosen_owner[:, None] == device_ids[None, :], axis=0)
    queries = suffix_query[0].reshape(slots, head_count, HEAD_DIM)
    normed_prefix = normalize(prefix_hidden[0]).astype(jnp.bfloat16)
    fresh = jnp.dot(normed_prefix, kv_weight, preferred_element_type=jnp.float32).astype(
        jnp.bfloat16
    )
    my_stale = jnp.any(chosen_owner == my_device)
    local_kv = jnp.where(my_stale, fresh, prefix_keyval[0])
    skip_device = jnp.zeros_like(stale_device)
    gathered = lax.all_gather(local_kv, "dev", axis=0, tiled=True)
    prefix_count = gathered.shape[0]
    row_device = jnp.arange(prefix_count, dtype=jnp.int32) // block_rows
    skipped = jnp.any((row_device[:, None] == device_ids[None, :]) & skip_device[None, :], axis=1)
    state = (
        jnp.full((head_count, slots), NEGATIVE, jnp.float32),
        jnp.zeros((head_count, slots), jnp.float32),
        jnp.zeros((slots, head_count, HEAD_DIM), jnp.float32),
    )
    key_block = 512 if prefix_count % 512 == 0 else prefix_count
    for block_start in range(0, prefix_count, key_block):
        kept = jnp.logical_not(skipped[block_start : block_start + key_block])
        allowed = jnp.broadcast_to(kept[None, :], (slots, key_block))
        state = absorb(state, queries, gathered[block_start : block_start + key_block], allowed)
    positions = jnp.arange(slots, dtype=jnp.int32)
    causal = (positions[None, :] <= positions[:, None]) & (positions[None, :] < my_length)
    state = absorb(state, queries, suffix_keyval[0], causal)
    final_top, final_total, accumulated = state
    attended = (
        (accumulated / jnp.transpose(final_total)[:, :, None])
        .reshape(slots, width_att)
        .astype(jnp.bfloat16)
    )
    projected = jnp.dot(attended, out_weight, preferred_element_type=jnp.float32)
    residual = suffix_x[0].astype(jnp.float32) + projected
    normed = normalize(residual).astype(jnp.bfloat16)
    group_count = lax.axis_size("group")
    hidden_part = fc_weight.shape[1]
    both = jnp.stack([fc_weight.T, proj_weight])
    keep = hidden_part * 3 // 4
    if ring_plan is None or keep == 0:
        banks = [lax.all_gather(both, "dev", axis=1)]
    else:
        banks = [
            ring_gather(both[:, keep:], *ring_plan),
            lax.all_gather(both[:, :keep], "dev", axis=1),
        ]

    def feed(rows_in):
        total = None
        for bank in banks:
            fc_rows = bank[0].reshape(-1, both.shape[2])
            proj_rows = bank[1].reshape(-1, both.shape[2])
            inner = lax.dot_general(
                rows_in, fc_rows, (((1,), (1,)), ((), ())), preferred_element_type=jnp.float32
            )
            activated = jax.nn.gelu(inner, approximate=True).astype(jnp.bfloat16)
            part = jnp.dot(activated, proj_rows, preferred_element_type=jnp.float32)
            total = part if total is None else total + part
        return total

    returned = []
    for shift in range(1, group_count):
        there = [(g, (g + shift) % group_count) for g in range(group_count)]
        back = [(g, (g - shift) % group_count) for g in range(group_count)]
        partner_normed = lax.ppermute(normed, "group", there)
        partner_feed = feed(partner_normed).astype(jnp.bfloat16)
        returned.append(lax.ppermute(partner_feed, "group", back))
    summed = lax.optimization_barrier(residual + feed(normed))
    for part in returned:
        summed = summed + part.astype(jnp.float32)
    live = positions[:, None] < my_length
    return jnp.where(live, summed, 0.0).astype(jnp.bfloat16)[None]


def solution(mesh):
    return jax.shard_map(
        functools.partial(per_device, plan_ring(mesh)),
        mesh=mesh,
        in_specs=(
            P("group", "dev", None),
            P("group", "dev", None),
            P("group", "dev", None),
            P("group", "dev", None),
            P("group", "dev", None),
            P(),
            P(),
            P(None, ("group", "dev")),
            P(("group", "dev"), None),
            P("group", None),
            P("group", None),
            P("group", None),
            P("group", None),
        ),
        out_specs=P("group", "dev", None),
        check_vma=False,
    )
```

```python
import functools

import jax
import jax.numpy as jnp
from jax import lax
from jax.sharding import PartitionSpec as P

HEAD_DIM = 64


NEGATIVE = -1e30
EPSILON = 1e-05
SCORE_SCALE = 0.125


def normalize(values_in):
    values_in = values_in.astype(jnp.float32)
    average = jnp.mean(values_in, axis=-1, keepdims=True)
    centered = values_in - average
    variance = jnp.mean(centered * centered, axis=-1, keepdims=True)
    return centered / jnp.sqrt(variance + EPSILON)


def absorb(state, queries, keyval, allowed):
    running_top, running_total, accumulated = state
    head_count = queries.shape[1]
    head_size = queries.shape[2]
    row_count = keyval.shape[0]
    width_att = head_count * head_size
    key_rows = keyval[:, :width_att].reshape(row_count, head_count, head_size)
    val_rows = keyval[:, width_att:].reshape(row_count, head_count, head_size)
    scores = (
        jnp.einsum("qhd,khd->hqk", queries, key_rows, preferred_element_type=jnp.float32)
        * SCORE_SCALE
    )
    scores = jnp.where(allowed[None], scores, NEGATIVE)
    new_top = jnp.maximum(running_top, jnp.max(scores, axis=-1))
    factor = jnp.exp(running_top - new_top)
    weights = jnp.where(allowed[None], jnp.exp(scores - new_top[:, :, None]), 0.0)
    running_total = running_total * factor + jnp.sum(weights, axis=-1)
    weights_low = weights.astype(jnp.bfloat16)
    update = jnp.einsum("hqk,khd->qhd", weights_low, val_rows, preferred_element_type=jnp.float32)
    accumulated = accumulated * jnp.transpose(factor)[:, :, None] + update
    return (new_top, running_total, accumulated)


def ring_gather(shard, forward, backward, swap, steps_forward, steps_backward):
    pieces = [shard]
    ahead = shard
    behind = shard
    for step in range(steps_forward):
        ahead = lax.ppermute(ahead, "dev", forward)
        pieces.append(ahead)
        if step < steps_backward:
            behind = lax.ppermute(behind, "dev", backward)
            pieces.append(behind)
    pieces = pieces + [lax.ppermute(piece, "dev", swap) for piece in pieces]
    return jnp.stack(pieces, axis=1)


def plan_ring(mesh):
    devices = mesh.devices
    device_count = devices.shape[1]
    if device_count % 2 or device_count < 4:
        return None
    chip_count = device_count // 2
    try:
        grids = []
        for row in devices:
            coords = [tuple(row[2 * k].coords) for k in range(chip_count)]
            if any(tuple(row[2 * k + 1].coords) != coords[k] for k in range(chip_count)):
                return None
            grids.append(coords)
    except AttributeError:
        return None
    coords = grids[0]
    varying = [axis for axis in range(len(coords[0])) if len({c[axis] for c in coords}) > 1]
    if len(varying) != 2:
        return None
    long_axis, short_axis = varying
    if len({c[short_axis] for c in coords}) != 2:
        long_axis, short_axis = short_axis, long_axis
    if len({c[short_axis] for c in coords}) != 2:
        return None
    low, high = sorted({c[short_axis] for c in coords})
    along = sorted({c[long_axis] for c in coords})
    place = {(c[short_axis], c[long_axis]): k for k, c in enumerate(coords)}
    if len(place) != chip_count:
        return None
    cycle = [place[(low, a)] for a in along] + [place[(high, a)] for a in reversed(along)]
    for coords_g in grids:
        for i in range(chip_count):
            first = coords_g[cycle[i]]
            second = coords_g[cycle[(i + 1) % chip_count]]
            if sum(abs(p - q) for p, q in zip(first, second)) != 1:
                return None
    after = {cycle[i]: cycle[(i + 1) % chip_count] for i in range(chip_count)}
    before = {cycle[i]: cycle[(i - 1) % chip_count] for i in range(chip_count)}
    forward = [(2 * k + c, 2 * after[k] + c) for k in range(chip_count) for c in range(2)]
    backward = [(2 * k + c, 2 * before[k] + c) for k in range(chip_count) for c in range(2)]
    swap = [(2 * k + c, 2 * k + 1 - c) for k in range(chip_count) for c in range(2)]
    steps_forward = chip_count // 2
    return forward, backward, swap, steps_forward, chip_count - 1 - steps_forward


def per_device(
    ring_plan,
    suffix_x,
    suffix_query,
    suffix_keyval,
    prefix_keyval,
    prefix_hidden,
    kv_weight,
    out_weight,
    fc_weight,
    proj_weight,
    lengths,
    placement,
    owners,
    recompute,
):
    device_count = lax.axis_size("dev")
    my_device = lax.axis_index("dev")
    slots = suffix_x.shape[1]
    block_rows = prefix_keyval.shape[1]
    width_att = suffix_query.shape[2]
    head_count = width_att // HEAD_DIM
    device_ids = jnp.arange(device_count, dtype=jnp.int32)
    hits = placement[0][:, None] == device_ids[None, :]
    device_length = jnp.sum(jnp.where(hits, lengths[0][:, None], 0), axis=0)
    my_length = jnp.sum(jnp.where(device_ids == my_device, device_length, 0))
    block_ids = jnp.arange(owners.shape[1], dtype=jnp.int32)
    chosen = recompute[0]
    chosen_owner = jnp.sum(
        jnp.where(chosen[:, None] == block_ids[None, :], owners[0][None, :], 0), axis=1
    )
    stale_device = jnp.any(chosen_owner[:, None] == device_ids[None, :], axis=0)
    queries = suffix_query[0].reshape(slots, head_count, HEAD_DIM)
    normed_prefix = normalize(prefix_hidden[0]).astype(jnp.bfloat16)
    fresh = jnp.dot(normed_prefix, kv_weight, preferred_element_type=jnp.float32).astype(
        jnp.bfloat16
    )
    my_stale = jnp.any(chosen_owner == my_device)
    local_kv = jnp.where(my_stale, fresh, prefix_keyval[0])
    skip_device = jnp.zeros_like(stale_device)
    gathered = lax.all_gather(local_kv, "dev", axis=0, tiled=True)
    prefix_count = gathered.shape[0]
    row_device = jnp.arange(prefix_count, dtype=jnp.int32) // block_rows
    skipped = jnp.any((row_device[:, None] == device_ids[None, :]) & skip_device[None, :], axis=1)
    state = (
        jnp.full((head_count, slots), NEGATIVE, jnp.float32),
        jnp.zeros((head_count, slots), jnp.float32),
        jnp.zeros((slots, head_count, HEAD_DIM), jnp.float32),
    )
    key_block = 512 if prefix_count % 512 == 0 else prefix_count
    for block_start in range(0, prefix_count, key_block):
        kept = jnp.logical_not(skipped[block_start : block_start + key_block])
        allowed = jnp.broadcast_to(kept[None, :], (slots, key_block))
        state = absorb(state, queries, gathered[block_start : block_start + key_block], allowed)
    positions = jnp.arange(slots, dtype=jnp.int32)
    causal = (positions[None, :] <= positions[:, None]) & (positions[None, :] < my_length)
    state = absorb(state, queries, suffix_keyval[0], causal)
    final_top, final_total, accumulated = state
    attended = (
        (accumulated / jnp.transpose(final_total)[:, :, None])
        .reshape(slots, width_att)
        .astype(jnp.bfloat16)
    )
    projected = jnp.dot(attended, out_weight, preferred_element_type=jnp.float32)
    residual = suffix_x[0].astype(jnp.float32) + projected
    normed = normalize(residual).astype(jnp.bfloat16)
    group_count = lax.axis_size("group")
    hidden_part = fc_weight.shape[1]
    both = jnp.stack([fc_weight.T, proj_weight])
    keep = hidden_part * 4 // 5 // 16 * 16
    if ring_plan is None or keep == 0:
        banks = [lax.all_gather(both, "dev", axis=1)]
    else:
        banks = [
            ring_gather(both[:, keep:], *ring_plan),
            lax.all_gather(both[:, :keep], "dev", axis=1),
        ]

    def feed(rows_in):
        total = None
        for bank in banks:
            if bank.ndim == 4 and bank is banks[0] and len(banks) > 1:
                inner = jnp.einsum(
                    "td,shd->tsh", rows_in, bank[0], preferred_element_type=jnp.float32
                )
                activated = jax.nn.gelu(inner, approximate=True).astype(jnp.bfloat16)
                part = jnp.einsum(
                    "tsh,shd->td", activated, bank[1], preferred_element_type=jnp.float32
                )
            else:
                fc_rows = bank[0].reshape(-1, both.shape[2])
                proj_rows = bank[1].reshape(-1, both.shape[2])
                inner = lax.dot_general(
                    rows_in, fc_rows, (((1,), (1,)), ((), ())), preferred_element_type=jnp.float32
                )
                activated = jax.nn.gelu(inner, approximate=True).astype(jnp.bfloat16)
                part = jnp.dot(activated, proj_rows, preferred_element_type=jnp.float32)
            total = part if total is None else total + part
        return total

    returned = []
    for shift in range(1, group_count):
        there = [(g, (g + shift) % group_count) for g in range(group_count)]
        back = [(g, (g - shift) % group_count) for g in range(group_count)]
        partner_normed = lax.ppermute(normed, "group", there)
        partner_feed = feed(partner_normed).astype(jnp.bfloat16)
        returned.append(lax.ppermute(partner_feed, "group", back))
    summed = lax.optimization_barrier(residual + feed(normed))
    for part in returned:
        summed = summed + part.astype(jnp.float32)
    live = positions[:, None] < my_length
    return jnp.where(live, summed, 0.0).astype(jnp.bfloat16)[None]


def solution(mesh):
    return jax.shard_map(
        functools.partial(per_device, plan_ring(mesh)),
        mesh=mesh,
        in_specs=(
            P("group", "dev", None),
            P("group", "dev", None),
            P("group", "dev", None),
            P("group", "dev", None),
            P("group", "dev", None),
            P(),
            P(),
            P(None, ("group", "dev")),
            P(("group", "dev"), None),
            P("group", None),
            P("group", None),
            P("group", None),
            P("group", None),
        ),
        out_specs=P("group", "dev", None),
        check_vma=False,
    )
```

```python
import functools

import jax
import jax.numpy as jnp
from jax import lax
from jax.sharding import PartitionSpec as P

HEAD_DIM = 64


NEGATIVE = -1e30
EPSILON = 1e-05
SCORE_SCALE = 0.125


def normalize(values_in):
    values_in = values_in.astype(jnp.float32)
    average = jnp.mean(values_in, axis=-1, keepdims=True)
    centered = values_in - average
    variance = jnp.mean(centered * centered, axis=-1, keepdims=True)
    return centered / jnp.sqrt(variance + EPSILON)


def absorb(state, queries, keyval, allowed):
    running_top, running_total, accumulated = state
    head_count = queries.shape[1]
    head_size = queries.shape[2]
    row_count = keyval.shape[0]
    width_att = head_count * head_size
    key_rows = keyval[:, :width_att].reshape(row_count, head_count, head_size)
    val_rows = keyval[:, width_att:].reshape(row_count, head_count, head_size)
    scores = (
        jnp.einsum("qhd,khd->hqk", queries, key_rows, preferred_element_type=jnp.float32)
        * SCORE_SCALE
    )
    scores = jnp.where(allowed[None], scores, NEGATIVE)
    new_top = jnp.maximum(running_top, jnp.max(scores, axis=-1))
    factor = jnp.exp(running_top - new_top)
    weights = jnp.where(allowed[None], jnp.exp(scores - new_top[:, :, None]), 0.0)
    running_total = running_total * factor + jnp.sum(weights, axis=-1)
    weights_low = weights.astype(jnp.bfloat16)
    update = jnp.einsum("hqk,khd->qhd", weights_low, val_rows, preferred_element_type=jnp.float32)
    accumulated = accumulated * jnp.transpose(factor)[:, :, None] + update
    return (new_top, running_total, accumulated)


def ring_issue(state, plan):
    forward, backward, full_steps, split = plan[0], plan[1], plan[3], plan[4]
    ahead, behind, pieces, done = state
    if done < full_steps:
        return lax.ppermute(ahead, "dev", forward), lax.ppermute(behind, "dev", backward)
    if done == full_steps and split:
        return lax.ppermute(ahead, "dev", forward), None
    return None


def ring_land(state, plan, sent, tie):
    ahead, behind, pieces, done = state
    if sent is None:
        return state, tie
    first, second = sent
    if second is None:
        tie, first = lax.optimization_barrier((tie, first))
        return (first, behind, pieces + [first], done + 1), tie
    tie, first, second = lax.optimization_barrier((tie, first, second))
    return (first, second, pieces + [first, second], done + 1), tie


def ring_step(state, plan, tie):
    return ring_land(state, plan, ring_issue(state, plan), tie)


def ring_finish(state, plan):
    swap = plan[2]
    while state[3] <= plan[3]:
        state, _ = ring_step(state, plan, jnp.zeros((), jnp.float32))
    pieces = state[2]
    pieces = pieces + [lax.ppermute(piece, "dev", swap) for piece in pieces]
    return jnp.stack(pieces, axis=1)


def plan_ring(mesh):
    devices = mesh.devices
    device_count = devices.shape[1]
    if device_count % 2 or device_count < 4:
        return None
    chip_count = device_count // 2
    try:
        grids = []
        for row in devices:
            coords = [tuple(row[2 * k].coords) for k in range(chip_count)]
            if any(tuple(row[2 * k + 1].coords) != coords[k] for k in range(chip_count)):
                return None
            grids.append(coords)
    except AttributeError:
        return None
    coords = grids[0]
    varying = [axis for axis in range(len(coords[0])) if len({c[axis] for c in coords}) > 1]
    if len(varying) != 2:
        return None
    long_axis, short_axis = varying
    if len({c[short_axis] for c in coords}) != 2:
        long_axis, short_axis = short_axis, long_axis
    if len({c[short_axis] for c in coords}) != 2:
        return None
    low, high = sorted({c[short_axis] for c in coords})
    along = sorted({c[long_axis] for c in coords})
    place = {(c[short_axis], c[long_axis]): k for k, c in enumerate(coords)}
    if len(place) != chip_count:
        return None
    cycle = [place[(low, a)] for a in along] + [place[(high, a)] for a in reversed(along)]
    for coords_g in grids:
        for i in range(chip_count):
            first = coords_g[cycle[i]]
            second = coords_g[cycle[(i + 1) % chip_count]]
            if sum(abs(p - q) for p, q in zip(first, second)) != 1:
                return None
    after = {cycle[i]: cycle[(i + 1) % chip_count] for i in range(chip_count)}
    before = {cycle[i]: cycle[(i - 1) % chip_count] for i in range(chip_count)}
    forward = [(2 * k + c, 2 * after[k] + c) for k in range(chip_count) for c in range(2)]
    backward = [(2 * k + c, 2 * before[k] + c) for k in range(chip_count) for c in range(2)]
    swap = [(2 * k + c, 2 * k + 1 - c) for k in range(chip_count) for c in range(2)]
    full_steps = (chip_count - 1) // 2
    return forward, backward, swap, full_steps, chip_count % 2 == 0


def per_device(
    ring_plan,
    suffix_x,
    suffix_query,
    suffix_keyval,
    prefix_keyval,
    prefix_hidden,
    kv_weight,
    out_weight,
    fc_weight,
    proj_weight,
    lengths,
    placement,
    owners,
    recompute,
):
    device_count = lax.axis_size("dev")
    my_device = lax.axis_index("dev")
    slots = suffix_x.shape[1]
    block_rows = prefix_keyval.shape[1]
    width_att = suffix_query.shape[2]
    head_count = width_att // HEAD_DIM
    device_ids = jnp.arange(device_count, dtype=jnp.int32)
    hits = placement[0][:, None] == device_ids[None, :]
    device_length = jnp.sum(jnp.where(hits, lengths[0][:, None], 0), axis=0)
    my_length = jnp.sum(jnp.where(device_ids == my_device, device_length, 0))
    block_ids = jnp.arange(owners.shape[1], dtype=jnp.int32)
    chosen = recompute[0]
    chosen_owner = jnp.sum(
        jnp.where(chosen[:, None] == block_ids[None, :], owners[0][None, :], 0), axis=1
    )
    stale_device = jnp.any(chosen_owner[:, None] == device_ids[None, :], axis=0)
    queries = suffix_query[0].reshape(slots, head_count, HEAD_DIM)
    normed_prefix = normalize(prefix_hidden[0]).astype(jnp.bfloat16)
    fresh = jnp.dot(normed_prefix, kv_weight, preferred_element_type=jnp.float32).astype(
        jnp.bfloat16
    )
    my_stale = jnp.any(chosen_owner == my_device)
    local_kv = jnp.where(my_stale, fresh, prefix_keyval[0])
    skip_device = jnp.zeros_like(stale_device)
    both = jnp.stack([fc_weight.T, proj_weight])
    hidden_part = fc_weight.shape[1]
    keep = hidden_part * 4 // 5 // 16 * 16
    use_ring = ring_plan is not None and keep > 0
    if use_ring:
        ring = (both[:, keep:], both[:, keep:], [both[:, keep:]], 0)
        ring, local_kv = ring_step(ring, ring_plan, local_kv)
        sent = ring_issue(ring, ring_plan)
    gathered = lax.all_gather(local_kv, "dev", axis=0, tiled=True)
    if use_ring:
        ring, gathered = ring_land(ring, ring_plan, sent, gathered)
    prefix_count = gathered.shape[0]
    row_device = jnp.arange(prefix_count, dtype=jnp.int32) // block_rows
    skipped = jnp.any((row_device[:, None] == device_ids[None, :]) & skip_device[None, :], axis=1)
    state = (
        jnp.full((head_count, slots), NEGATIVE, jnp.float32),
        jnp.zeros((head_count, slots), jnp.float32),
        jnp.zeros((slots, head_count, HEAD_DIM), jnp.float32),
    )
    key_block = 512 if prefix_count % 512 == 0 else prefix_count
    for block_start in range(0, prefix_count, key_block):
        kept = jnp.logical_not(skipped[block_start : block_start + key_block])
        allowed = jnp.broadcast_to(kept[None, :], (slots, key_block))
        state = absorb(state, queries, gathered[block_start : block_start + key_block], allowed)
    positions = jnp.arange(slots, dtype=jnp.int32)
    causal = (positions[None, :] <= positions[:, None]) & (positions[None, :] < my_length)
    state = absorb(state, queries, suffix_keyval[0], causal)
    final_top, final_total, accumulated = state
    attended = (
        (accumulated / jnp.transpose(final_total)[:, :, None])
        .reshape(slots, width_att)
        .astype(jnp.bfloat16)
    )
    projected = jnp.dot(attended, out_weight, preferred_element_type=jnp.float32)
    residual = suffix_x[0].astype(jnp.float32) + projected
    normed = normalize(residual).astype(jnp.bfloat16)
    if use_ring:
        ring, normed = ring_step(ring, ring_plan, normed)
    group_count = lax.axis_size("group")
    if not use_ring:
        banks = [lax.all_gather(both, "dev", axis=1)]
    else:
        banks = [
            ring_finish(ring, ring_plan),
            lax.all_gather(both[:, :keep], "dev", axis=1),
        ]

    def feed(rows_in):
        total = None
        for bank in banks:
            if bank.ndim == 4 and bank is banks[0] and len(banks) > 1:
                inner = jnp.einsum(
                    "td,shd->tsh", rows_in, bank[0], preferred_element_type=jnp.float32
                )
                activated = jax.nn.gelu(inner, approximate=True).astype(jnp.bfloat16)
                part = jnp.einsum(
                    "tsh,shd->td", activated, bank[1], preferred_element_type=jnp.float32
                )
            else:
                fc_rows = bank[0].reshape(-1, both.shape[2])
                proj_rows = bank[1].reshape(-1, both.shape[2])
                inner = lax.dot_general(
                    rows_in, fc_rows, (((1,), (1,)), ((), ())), preferred_element_type=jnp.float32
                )
                activated = jax.nn.gelu(inner, approximate=True).astype(jnp.bfloat16)
                part = jnp.dot(activated, proj_rows, preferred_element_type=jnp.float32)
            total = part if total is None else total + part
        return total

    returned = []
    for shift in range(1, group_count):
        there = [(g, (g + shift) % group_count) for g in range(group_count)]
        back = [(g, (g - shift) % group_count) for g in range(group_count)]
        partner_normed = lax.ppermute(normed, "group", there)
        partner_feed = feed(partner_normed).astype(jnp.bfloat16)
        returned.append(lax.ppermute(partner_feed, "group", back))
    summed = lax.optimization_barrier(residual + feed(normed))
    for part in returned:
        summed = summed + part.astype(jnp.float32)
    live = positions[:, None] < my_length
    return jnp.where(live, summed, 0.0).astype(jnp.bfloat16)[None]


def solution(mesh):
    return jax.shard_map(
        functools.partial(per_device, plan_ring(mesh)),
        mesh=mesh,
        in_specs=(
            P("group", "dev", None),
            P("group", "dev", None),
            P("group", "dev", None),
            P("group", "dev", None),
            P("group", "dev", None),
            P(),
            P(),
            P(None, ("group", "dev")),
            P(("group", "dev"), None),
            P("group", None),
            P("group", None),
            P("group", None),
            P("group", None),
        ),
        out_specs=P("group", "dev", None),
        check_vma=False,
    )
```

```python
import functools

import jax
import jax.numpy as jnp
from jax import lax
from jax.sharding import PartitionSpec as P

HEAD_DIM = 64


NEGATIVE = -1e30
EPSILON = 1e-05
SCORE_SCALE = 0.125


def normalize(values_in):
    values_in = values_in.astype(jnp.float32)
    average = jnp.mean(values_in, axis=-1, keepdims=True)
    centered = values_in - average
    variance = jnp.mean(centered * centered, axis=-1, keepdims=True)
    return centered / jnp.sqrt(variance + EPSILON)


def absorb(state, queries, keyval, allowed):
    running_top, running_total, accumulated = state
    head_count = queries.shape[1]
    head_size = queries.shape[2]
    row_count = keyval.shape[0]
    width_att = head_count * head_size
    key_rows = keyval[:, :width_att].reshape(row_count, head_count, head_size)
    val_rows = keyval[:, width_att:].reshape(row_count, head_count, head_size)
    scores = (
        jnp.einsum("qhd,khd->hqk", queries, key_rows, preferred_element_type=jnp.float32)
        * SCORE_SCALE
    )
    scores = jnp.where(allowed[None], scores, NEGATIVE)
    new_top = jnp.maximum(running_top, jnp.max(scores, axis=-1))
    factor = jnp.exp(running_top - new_top)
    weights = jnp.where(allowed[None], jnp.exp(scores - new_top[:, :, None]), 0.0)
    running_total = running_total * factor + jnp.sum(weights, axis=-1)
    weights_low = weights.astype(jnp.bfloat16)
    update = jnp.einsum("hqk,khd->qhd", weights_low, val_rows, preferred_element_type=jnp.float32)
    accumulated = accumulated * jnp.transpose(factor)[:, :, None] + update
    return (new_top, running_total, accumulated)


def ring_issue(state, plan):
    forward, backward, full_steps, split = plan[0], plan[1], plan[3], plan[4]
    ahead, behind, pieces, done = state
    if done < full_steps:
        return lax.ppermute(ahead, "dev", forward), lax.ppermute(behind, "dev", backward)
    if done == full_steps and split:
        return lax.ppermute(ahead, "dev", forward), None
    return None


def ring_land(state, plan, sent, tie):
    ahead, behind, pieces, done = state
    if sent is None:
        return state, tie
    first, second = sent
    if second is None:
        tie, first = lax.optimization_barrier((tie, first))
        return (first, behind, pieces + [first], done + 1), tie
    tie, first, second = lax.optimization_barrier((tie, first, second))
    return (first, second, pieces + [first, second], done + 1), tie


def ring_step(state, plan, tie):
    return ring_land(state, plan, ring_issue(state, plan), tie)


def ring_finish(state, plan):
    swap = plan[2]
    while state[3] <= plan[3]:
        state, _ = ring_step(state, plan, jnp.zeros((), jnp.float32))
    pieces = state[2]
    pieces = pieces + [lax.ppermute(piece, "dev", swap) for piece in pieces]
    return jnp.stack(pieces, axis=1)


def plan_ring(mesh):
    devices = mesh.devices
    device_count = devices.shape[1]
    if device_count % 2 or device_count < 4:
        return None
    chip_count = device_count // 2
    try:
        grids = []
        for row in devices:
            coords = [tuple(row[2 * k].coords) for k in range(chip_count)]
            if any(tuple(row[2 * k + 1].coords) != coords[k] for k in range(chip_count)):
                return None
            grids.append(coords)
    except AttributeError:
        return None
    coords = grids[0]
    varying = [axis for axis in range(len(coords[0])) if len({c[axis] for c in coords}) > 1]
    if len(varying) != 2:
        return None
    long_axis, short_axis = varying
    if len({c[short_axis] for c in coords}) != 2:
        long_axis, short_axis = short_axis, long_axis
    if len({c[short_axis] for c in coords}) != 2:
        return None
    low, high = sorted({c[short_axis] for c in coords})
    along = sorted({c[long_axis] for c in coords})
    place = {(c[short_axis], c[long_axis]): k for k, c in enumerate(coords)}
    if len(place) != chip_count:
        return None
    cycle = [place[(low, a)] for a in along] + [place[(high, a)] for a in reversed(along)]
    for coords_g in grids:
        for i in range(chip_count):
            first = coords_g[cycle[i]]
            second = coords_g[cycle[(i + 1) % chip_count]]
            if sum(abs(p - q) for p, q in zip(first, second)) != 1:
                return None
    after = {cycle[i]: cycle[(i + 1) % chip_count] for i in range(chip_count)}
    before = {cycle[i]: cycle[(i - 1) % chip_count] for i in range(chip_count)}
    forward = [(2 * k + c, 2 * after[k] + c) for k in range(chip_count) for c in range(2)]
    backward = [(2 * k + c, 2 * before[k] + c) for k in range(chip_count) for c in range(2)]
    swap = [(2 * k + c, 2 * k + 1 - c) for k in range(chip_count) for c in range(2)]
    full_steps = (chip_count - 1) // 2
    return forward, backward, swap, full_steps, chip_count % 2 == 0


def per_device(
    ring_plan,
    suffix_x,
    suffix_query,
    suffix_keyval,
    prefix_keyval,
    prefix_hidden,
    kv_weight,
    out_weight,
    fc_weight,
    proj_weight,
    lengths,
    placement,
    owners,
    recompute,
):
    device_count = lax.axis_size("dev")
    my_device = lax.axis_index("dev")
    slots = suffix_x.shape[1]
    block_rows = prefix_keyval.shape[1]
    width_att = suffix_query.shape[2]
    head_count = width_att // HEAD_DIM
    device_ids = jnp.arange(device_count, dtype=jnp.int32)
    hits = placement[0][:, None] == device_ids[None, :]
    device_length = jnp.sum(jnp.where(hits, lengths[0][:, None], 0), axis=0)
    my_length = jnp.sum(jnp.where(device_ids == my_device, device_length, 0))
    block_ids = jnp.arange(owners.shape[1], dtype=jnp.int32)
    chosen = recompute[0]
    chosen_owner = jnp.sum(
        jnp.where(chosen[:, None] == block_ids[None, :], owners[0][None, :], 0), axis=1
    )
    stale_device = jnp.any(chosen_owner[:, None] == device_ids[None, :], axis=0)
    queries = suffix_query[0].reshape(slots, head_count, HEAD_DIM)
    normed_prefix = normalize(prefix_hidden[0]).astype(jnp.bfloat16)
    fresh = jnp.dot(normed_prefix, kv_weight, preferred_element_type=jnp.float32).astype(
        jnp.bfloat16
    )
    my_stale = jnp.any(chosen_owner == my_device)
    local_kv = jnp.where(my_stale, fresh, prefix_keyval[0])
    skip_device = jnp.zeros_like(stale_device)
    both = jnp.stack([fc_weight.T, proj_weight])
    hidden_part = fc_weight.shape[1]
    keep = hidden_part * 4 // 5 // 16 * 16
    use_ring = ring_plan is not None and keep > 0
    if use_ring:
        ring = (both[:, keep:], both[:, keep:], [both[:, keep:]], 0)
        ring, local_kv = ring_step(ring, ring_plan, local_kv)
        sent = ring_issue(ring, ring_plan)
    gathered = lax.all_gather(local_kv, "dev", axis=0, tiled=True)
    if use_ring:
        ring, gathered = ring_land(ring, ring_plan, sent, gathered)
    prefix_count = gathered.shape[0]
    row_device = jnp.arange(prefix_count, dtype=jnp.int32) // block_rows
    skipped = jnp.any((row_device[:, None] == device_ids[None, :]) & skip_device[None, :], axis=1)
    state = (
        jnp.full((head_count, slots), NEGATIVE, jnp.float32),
        jnp.zeros((head_count, slots), jnp.float32),
        jnp.zeros((slots, head_count, HEAD_DIM), jnp.float32),
    )
    key_block = 512 if prefix_count % 512 == 0 else prefix_count
    for block_start in range(0, prefix_count, key_block):
        kept = jnp.logical_not(skipped[block_start : block_start + key_block])
        allowed = jnp.broadcast_to(kept[None, :], (slots, key_block))
        state = absorb(state, queries, gathered[block_start : block_start + key_block], allowed)
    positions = jnp.arange(slots, dtype=jnp.int32)
    causal = (positions[None, :] <= positions[:, None]) & (positions[None, :] < my_length)
    state = absorb(state, queries, suffix_keyval[0], causal)
    final_top, final_total, accumulated = state
    attended = (
        (accumulated / jnp.transpose(final_total)[:, :, None])
        .reshape(slots, width_att)
        .astype(jnp.bfloat16)
    )
    projected = jnp.dot(attended, out_weight, preferred_element_type=jnp.float32)
    residual = suffix_x[0].astype(jnp.float32) + projected
    normed = normalize(residual).astype(jnp.bfloat16)
    if use_ring:
        ring, _ = ring_step(ring, ring_plan, normed)
    group_count = lax.axis_size("group")
    if not use_ring:
        banks = [lax.all_gather(both, "dev", axis=1)]
    else:
        banks = [
            ring_finish(ring, ring_plan),
            lax.all_gather(both[:, :keep], "dev", axis=1),
        ]

    def feed(rows_in):
        total = None
        for bank in banks:
            if bank.ndim == 4 and bank is banks[0] and len(banks) > 1:
                inner = jnp.einsum(
                    "td,shd->tsh", rows_in, bank[0], preferred_element_type=jnp.float32
                )
                activated = jax.nn.gelu(inner, approximate=True).astype(jnp.bfloat16)
                part = jnp.einsum(
                    "tsh,shd->td", activated, bank[1], preferred_element_type=jnp.float32
                )
            else:
                fc_rows = bank[0].reshape(-1, both.shape[2])
                proj_rows = bank[1].reshape(-1, both.shape[2])
                inner = lax.dot_general(
                    rows_in, fc_rows, (((1,), (1,)), ((), ())), preferred_element_type=jnp.float32
                )
                activated = jax.nn.gelu(inner, approximate=True).astype(jnp.bfloat16)
                part = jnp.dot(activated, proj_rows, preferred_element_type=jnp.float32)
            total = part if total is None else total + part
        return total

    returned = []
    for shift in range(1, group_count):
        there = [(g, (g + shift) % group_count) for g in range(group_count)]
        back = [(g, (g - shift) % group_count) for g in range(group_count)]
        partner_normed = lax.ppermute(normed, "group", there)
        partner_feed = feed(partner_normed).astype(jnp.bfloat16)
        returned.append(lax.ppermute(partner_feed, "group", back))
    summed = lax.optimization_barrier(residual + feed(normed))
    for part in returned:
        summed = summed + part.astype(jnp.float32)
    live = positions[:, None] < my_length
    return jnp.where(live, summed, 0.0).astype(jnp.bfloat16)[None]


def solution(mesh):
    return jax.shard_map(
        functools.partial(per_device, plan_ring(mesh)),
        mesh=mesh,
        in_specs=(
            P("group", "dev", None),
            P("group", "dev", None),
            P("group", "dev", None),
            P("group", "dev", None),
            P("group", "dev", None),
            P(),
            P(),
            P(None, ("group", "dev")),
            P(("group", "dev"), None),
            P("group", None),
            P("group", None),
            P("group", None),
            P("group", None),
        ),
        out_specs=P("group", "dev", None),
        check_vma=False,
    )
```

```python
import functools

import jax
import jax.numpy as jnp
from jax import lax
from jax.sharding import PartitionSpec as P

HEAD_DIM = 64


NEGATIVE = -1e30
EPSILON = 1e-05
SCORE_SCALE = 0.125


def normalize(values_in):
    values_in = values_in.astype(jnp.float32)
    average = jnp.mean(values_in, axis=-1, keepdims=True)
    centered = values_in - average
    variance = jnp.mean(centered * centered, axis=-1, keepdims=True)
    return centered / jnp.sqrt(variance + EPSILON)


def absorb(state, queries, keyval, allowed):
    running_top, running_total, accumulated = state
    head_count = queries.shape[1]
    head_size = queries.shape[2]
    row_count = keyval.shape[0]
    width_att = head_count * head_size
    key_rows = keyval[:, :width_att].reshape(row_count, head_count, head_size)
    val_rows = keyval[:, width_att:].reshape(row_count, head_count, head_size)
    scores = (
        jnp.einsum("qhd,khd->hqk", queries, key_rows, preferred_element_type=jnp.float32)
        * SCORE_SCALE
    )
    scores = jnp.where(allowed[None], scores, NEGATIVE)
    new_top = jnp.maximum(running_top, jnp.max(scores, axis=-1))
    factor = jnp.exp(running_top - new_top)
    weights = jnp.where(allowed[None], jnp.exp(scores - new_top[:, :, None]), 0.0)
    running_total = running_total * factor + jnp.sum(weights, axis=-1)
    weights_low = weights.astype(jnp.bfloat16)
    update = jnp.einsum("hqk,khd->qhd", weights_low, val_rows, preferred_element_type=jnp.float32)
    accumulated = accumulated * jnp.transpose(factor)[:, :, None] + update
    return (new_top, running_total, accumulated)


def ring_issue(state, plan):
    forward, backward, full_steps, split = plan[0], plan[1], plan[3], plan[4]
    ahead, behind, pieces, done = state
    if done < full_steps:
        return lax.ppermute(ahead, "dev", forward), lax.ppermute(behind, "dev", backward)
    if done == full_steps and split:
        return lax.ppermute(ahead, "dev", forward), None
    return None


def ring_land(state, plan, sent, tie):
    ahead, behind, pieces, done = state
    if sent is None:
        return state, tie
    first, second = sent
    if second is None:
        tie, first = lax.optimization_barrier((tie, first))
        return (first, behind, pieces + [first], done + 1), tie
    tie, first, second = lax.optimization_barrier((tie, first, second))
    return (first, second, pieces + [first, second], done + 1), tie


def ring_step(state, plan, tie):
    return ring_land(state, plan, ring_issue(state, plan), tie)


def ring_finish(state, plan):
    swap = plan[2]
    while state[3] <= plan[3]:
        state, _ = ring_step(state, plan, jnp.zeros((), jnp.float32))
    mine = jnp.stack(state[2], axis=1)
    return jnp.concatenate([mine, lax.ppermute(mine, "dev", swap)], axis=1)


def plan_ring(mesh):
    devices = mesh.devices
    device_count = devices.shape[1]
    if device_count % 2 or device_count < 4:
        return None
    chip_count = device_count // 2
    try:
        grids = []
        for row in devices:
            coords = [tuple(row[2 * k].coords) for k in range(chip_count)]
            if any(tuple(row[2 * k + 1].coords) != coords[k] for k in range(chip_count)):
                return None
            grids.append(coords)
    except AttributeError:
        return None
    coords = grids[0]
    varying = [axis for axis in range(len(coords[0])) if len({c[axis] for c in coords}) > 1]
    if len(varying) != 2:
        return None
    long_axis, short_axis = varying
    if len({c[short_axis] for c in coords}) != 2:
        long_axis, short_axis = short_axis, long_axis
    if len({c[short_axis] for c in coords}) != 2:
        return None
    low, high = sorted({c[short_axis] for c in coords})
    along = sorted({c[long_axis] for c in coords})
    place = {(c[short_axis], c[long_axis]): k for k, c in enumerate(coords)}
    if len(place) != chip_count:
        return None
    cycle = [place[(low, a)] for a in along] + [place[(high, a)] for a in reversed(along)]
    for coords_g in grids:
        for i in range(chip_count):
            first = coords_g[cycle[i]]
            second = coords_g[cycle[(i + 1) % chip_count]]
            if sum(abs(p - q) for p, q in zip(first, second)) != 1:
                return None
    after = {cycle[i]: cycle[(i + 1) % chip_count] for i in range(chip_count)}
    before = {cycle[i]: cycle[(i - 1) % chip_count] for i in range(chip_count)}
    forward = [(2 * k + c, 2 * after[k] + c) for k in range(chip_count) for c in range(2)]
    backward = [(2 * k + c, 2 * before[k] + c) for k in range(chip_count) for c in range(2)]
    swap = [(2 * k + c, 2 * k + 1 - c) for k in range(chip_count) for c in range(2)]
    full_steps = (chip_count - 1) // 2
    return forward, backward, swap, full_steps, chip_count % 2 == 0


def per_device(
    ring_plan,
    suffix_x,
    suffix_query,
    suffix_keyval,
    prefix_keyval,
    prefix_hidden,
    kv_weight,
    out_weight,
    fc_weight,
    proj_weight,
    lengths,
    placement,
    owners,
    recompute,
):
    device_count = lax.axis_size("dev")
    my_device = lax.axis_index("dev")
    slots = suffix_x.shape[1]
    block_rows = prefix_keyval.shape[1]
    width_att = suffix_query.shape[2]
    head_count = width_att // HEAD_DIM
    device_ids = jnp.arange(device_count, dtype=jnp.int32)
    hits = placement[0][:, None] == device_ids[None, :]
    device_length = jnp.sum(jnp.where(hits, lengths[0][:, None], 0), axis=0)
    my_length = jnp.sum(jnp.where(device_ids == my_device, device_length, 0))
    block_ids = jnp.arange(owners.shape[1], dtype=jnp.int32)
    chosen = recompute[0]
    chosen_owner = jnp.sum(
        jnp.where(chosen[:, None] == block_ids[None, :], owners[0][None, :], 0), axis=1
    )
    stale_device = jnp.any(chosen_owner[:, None] == device_ids[None, :], axis=0)
    queries = suffix_query[0].reshape(slots, head_count, HEAD_DIM)
    normed_prefix = normalize(prefix_hidden[0]).astype(jnp.bfloat16)
    fresh = jnp.dot(normed_prefix, kv_weight, preferred_element_type=jnp.float32).astype(
        jnp.bfloat16
    )
    my_stale = jnp.any(chosen_owner == my_device)
    local_kv = jnp.where(my_stale, fresh, prefix_keyval[0])
    skip_device = jnp.zeros_like(stale_device)
    both = jnp.stack([fc_weight.T, proj_weight])
    hidden_part = fc_weight.shape[1]
    keep = hidden_part * 4 // 5 // 16 * 16
    use_ring = ring_plan is not None and keep > 0
    if use_ring:
        ring = (both[:, keep:], both[:, keep:], [both[:, keep:]], 0)
        ring, local_kv = ring_step(ring, ring_plan, local_kv)
        sent = ring_issue(ring, ring_plan)
    gathered = lax.all_gather(local_kv, "dev", axis=0, tiled=True)
    if use_ring:
        ring, gathered = ring_land(ring, ring_plan, sent, gathered)
    prefix_count = gathered.shape[0]
    row_device = jnp.arange(prefix_count, dtype=jnp.int32) // block_rows
    skipped = jnp.any((row_device[:, None] == device_ids[None, :]) & skip_device[None, :], axis=1)
    state = (
        jnp.full((head_count, slots), NEGATIVE, jnp.float32),
        jnp.zeros((head_count, slots), jnp.float32),
        jnp.zeros((slots, head_count, HEAD_DIM), jnp.float32),
    )
    key_block = 512 if prefix_count % 512 == 0 else prefix_count
    for block_start in range(0, prefix_count, key_block):
        kept = jnp.logical_not(skipped[block_start : block_start + key_block])
        allowed = jnp.broadcast_to(kept[None, :], (slots, key_block))
        state = absorb(state, queries, gathered[block_start : block_start + key_block], allowed)
    positions = jnp.arange(slots, dtype=jnp.int32)
    causal = (positions[None, :] <= positions[:, None]) & (positions[None, :] < my_length)
    state = absorb(state, queries, suffix_keyval[0], causal)
    final_top, final_total, accumulated = state
    attended = (
        (accumulated / jnp.transpose(final_total)[:, :, None])
        .reshape(slots, width_att)
        .astype(jnp.bfloat16)
    )
    projected = jnp.dot(attended, out_weight, preferred_element_type=jnp.float32)
    residual = suffix_x[0].astype(jnp.float32) + projected
    normed = normalize(residual).astype(jnp.bfloat16)
    group_count = lax.axis_size("group")
    if not use_ring:
        banks = [lax.all_gather(both, "dev", axis=1)]
    else:
        banks = [
            ring_finish(ring, ring_plan),
            lax.all_gather(both[:, :keep], "dev", axis=1),
        ]

    def feed(rows_in):
        total = None
        for bank in banks:
            if bank.ndim == 4 and bank is banks[0] and len(banks) > 1:
                inner = jnp.einsum(
                    "td,shd->tsh", rows_in, bank[0], preferred_element_type=jnp.float32
                )
                activated = jax.nn.gelu(inner, approximate=True).astype(jnp.bfloat16)
                part = jnp.einsum(
                    "tsh,shd->td", activated, bank[1], preferred_element_type=jnp.float32
                )
            else:
                fc_rows = bank[0].reshape(-1, both.shape[2])
                proj_rows = bank[1].reshape(-1, both.shape[2])
                inner = lax.dot_general(
                    rows_in, fc_rows, (((1,), (1,)), ((), ())), preferred_element_type=jnp.float32
                )
                activated = jax.nn.gelu(inner, approximate=True).astype(jnp.bfloat16)
                part = jnp.dot(activated, proj_rows, preferred_element_type=jnp.float32)
            total = part if total is None else total + part
        return total

    returned = []
    for shift in range(1, group_count):
        there = [(g, (g + shift) % group_count) for g in range(group_count)]
        back = [(g, (g - shift) % group_count) for g in range(group_count)]
        partner_normed = lax.ppermute(normed, "group", there)
        partner_feed = feed(partner_normed).astype(jnp.bfloat16)
        returned.append(lax.ppermute(partner_feed, "group", back))
    summed = lax.optimization_barrier(residual + feed(normed))
    for part in returned:
        summed = summed + part.astype(jnp.float32)
    live = positions[:, None] < my_length
    return jnp.where(live, summed, 0.0).astype(jnp.bfloat16)[None]


def solution(mesh):
    return jax.shard_map(
        functools.partial(per_device, plan_ring(mesh)),
        mesh=mesh,
        in_specs=(
            P("group", "dev", None),
            P("group", "dev", None),
            P("group", "dev", None),
            P("group", "dev", None),
            P("group", "dev", None),
            P(),
            P(),
            P(None, ("group", "dev")),
            P(("group", "dev"), None),
            P("group", None),
            P("group", None),
            P("group", None),
            P("group", None),
        ),
        out_specs=P("group", "dev", None),
        check_vma=False,
    )
```

```python
import functools

import jax
import jax.numpy as jnp
from jax import lax
from jax.sharding import PartitionSpec as P

HEAD_DIM = 64


NEGATIVE = -1e30
EPSILON = 1e-05
SCORE_SCALE = 0.125


def normalize(values_in):
    values_in = values_in.astype(jnp.float32)
    average = jnp.mean(values_in, axis=-1, keepdims=True)
    centered = values_in - average
    variance = jnp.mean(centered * centered, axis=-1, keepdims=True)
    return centered / jnp.sqrt(variance + EPSILON)


def absorb(state, queries, keyval, allowed):
    running_top, running_total, accumulated = state
    head_count = queries.shape[1]
    head_size = queries.shape[2]
    row_count = keyval.shape[0]
    width_att = head_count * head_size
    key_rows = keyval[:, :width_att].reshape(row_count, head_count, head_size)
    val_rows = keyval[:, width_att:].reshape(row_count, head_count, head_size)
    scores = (
        jnp.einsum("qhd,khd->hqk", queries, key_rows, preferred_element_type=jnp.float32)
        * SCORE_SCALE
    )
    scores = jnp.where(allowed[None], scores, NEGATIVE)
    new_top = jnp.maximum(running_top, jnp.max(scores, axis=-1))
    factor = jnp.exp(running_top - new_top)
    weights = jnp.where(allowed[None], jnp.exp(scores - new_top[:, :, None]), 0.0)
    running_total = running_total * factor + jnp.sum(weights, axis=-1)
    weights_low = weights.astype(jnp.bfloat16)
    update = jnp.einsum("hqk,khd->qhd", weights_low, val_rows, preferred_element_type=jnp.float32)
    accumulated = accumulated * jnp.transpose(factor)[:, :, None] + update
    return (new_top, running_total, accumulated)


def ring_gather(shard, forward, backward, swap, steps_forward, steps_backward):
    pieces = [shard]
    ahead = shard
    behind = shard
    for step in range(steps_forward):
        ahead = lax.ppermute(ahead, "dev", forward)
        pieces.append(ahead)
        if step < steps_backward:
            behind = lax.ppermute(behind, "dev", backward)
            pieces.append(behind)
    pieces = pieces + [lax.ppermute(piece, "dev", swap) for piece in pieces]
    return jnp.stack(pieces, axis=1)


def plan_ring(mesh):
    devices = mesh.devices
    device_count = devices.shape[1]
    if device_count % 2 or device_count < 4:
        return None
    chip_count = device_count // 2
    try:
        grids = []
        for row in devices:
            coords = [tuple(row[2 * k].coords) for k in range(chip_count)]
            if any(tuple(row[2 * k + 1].coords) != coords[k] for k in range(chip_count)):
                return None
            grids.append(coords)
    except AttributeError:
        return None
    coords = grids[0]
    varying = [axis for axis in range(len(coords[0])) if len({c[axis] for c in coords}) > 1]
    if len(varying) != 2:
        return None
    long_axis, short_axis = varying
    if len({c[short_axis] for c in coords}) != 2:
        long_axis, short_axis = short_axis, long_axis
    if len({c[short_axis] for c in coords}) != 2:
        return None
    low, high = sorted({c[short_axis] for c in coords})
    along = sorted({c[long_axis] for c in coords})
    place = {(c[short_axis], c[long_axis]): k for k, c in enumerate(coords)}
    if len(place) != chip_count:
        return None
    cycle = [place[(low, a)] for a in along] + [place[(high, a)] for a in reversed(along)]
    for coords_g in grids:
        for i in range(chip_count):
            first = coords_g[cycle[i]]
            second = coords_g[cycle[(i + 1) % chip_count]]
            if sum(abs(p - q) for p, q in zip(first, second)) != 1:
                return None
    after = {cycle[i]: cycle[(i + 1) % chip_count] for i in range(chip_count)}
    before = {cycle[i]: cycle[(i - 1) % chip_count] for i in range(chip_count)}
    forward = [(2 * k + c, 2 * after[k] + c) for k in range(chip_count) for c in range(2)]
    backward = [(2 * k + c, 2 * before[k] + c) for k in range(chip_count) for c in range(2)]
    swap = [(2 * k + c, 2 * k + 1 - c) for k in range(chip_count) for c in range(2)]
    steps_forward = chip_count // 2
    return forward, backward, swap, steps_forward, chip_count - 1 - steps_forward


def per_device(
    ring_plan,
    suffix_x,
    suffix_query,
    suffix_keyval,
    prefix_keyval,
    prefix_hidden,
    kv_weight,
    out_weight,
    fc_weight,
    proj_weight,
    lengths,
    placement,
    owners,
    recompute,
):
    device_count = lax.axis_size("dev")
    my_device = lax.axis_index("dev")
    slots = suffix_x.shape[1]
    block_rows = prefix_keyval.shape[1]
    width_att = suffix_query.shape[2]
    head_count = width_att // HEAD_DIM
    device_ids = jnp.arange(device_count, dtype=jnp.int32)
    hits = placement[0][:, None] == device_ids[None, :]
    device_length = jnp.sum(jnp.where(hits, lengths[0][:, None], 0), axis=0)
    my_length = jnp.sum(jnp.where(device_ids == my_device, device_length, 0))
    block_ids = jnp.arange(owners.shape[1], dtype=jnp.int32)
    chosen = recompute[0]
    chosen_owner = jnp.sum(
        jnp.where(chosen[:, None] == block_ids[None, :], owners[0][None, :], 0), axis=1
    )
    stale_device = jnp.any(chosen_owner[:, None] == device_ids[None, :], axis=0)
    queries = suffix_query[0].reshape(slots, head_count, HEAD_DIM)
    normed_prefix = normalize(prefix_hidden[0]).astype(jnp.bfloat16)
    fresh = jnp.dot(normed_prefix, kv_weight, preferred_element_type=jnp.float32).astype(
        jnp.bfloat16
    )
    my_stale = jnp.any(chosen_owner == my_device)
    local_kv = jnp.where(my_stale, fresh, prefix_keyval[0])
    skip_device = jnp.zeros_like(stale_device)
    gathered = lax.all_gather(local_kv, "dev", axis=0, tiled=True)
    prefix_count = gathered.shape[0]
    row_device = jnp.arange(prefix_count, dtype=jnp.int32) // block_rows
    skipped = jnp.any((row_device[:, None] == device_ids[None, :]) & skip_device[None, :], axis=1)
    state = (
        jnp.full((head_count, slots), NEGATIVE, jnp.float32),
        jnp.zeros((head_count, slots), jnp.float32),
        jnp.zeros((slots, head_count, HEAD_DIM), jnp.float32),
    )
    key_block = 512 if prefix_count % 512 == 0 else prefix_count
    for block_start in range(0, prefix_count, key_block):
        kept = jnp.logical_not(skipped[block_start : block_start + key_block])
        allowed = jnp.broadcast_to(kept[None, :], (slots, key_block))
        state = absorb(state, queries, gathered[block_start : block_start + key_block], allowed)
    positions = jnp.arange(slots, dtype=jnp.int32)
    causal = (positions[None, :] <= positions[:, None]) & (positions[None, :] < my_length)
    state = absorb(state, queries, suffix_keyval[0], causal)
    final_top, final_total, accumulated = state
    attended = (
        (accumulated / jnp.transpose(final_total)[:, :, None])
        .reshape(slots, width_att)
        .astype(jnp.bfloat16)
    )
    projected = jnp.dot(attended, out_weight, preferred_element_type=jnp.float32)
    residual = suffix_x[0].astype(jnp.float32) + projected
    normed = normalize(residual).astype(jnp.bfloat16)
    group_count = lax.axis_size("group")
    hidden_part = fc_weight.shape[1]
    both = jnp.stack([fc_weight.T, proj_weight])
    keep = (hidden_part - 8) // 16 * 16
    if ring_plan is None or keep == 0:
        banks = [lax.all_gather(both, "dev", axis=1)]
    else:
        banks = [
            ring_gather(both[:, keep:], *ring_plan),
            lax.all_gather(both[:, :keep], "dev", axis=1),
        ]

    def feed(rows_in):
        total = None
        for bank in banks:
            if bank.ndim == 4 and bank is banks[0] and len(banks) > 1:
                inner = jnp.einsum(
                    "td,shd->tsh", rows_in, bank[0], preferred_element_type=jnp.float32
                )
                activated = jax.nn.gelu(inner, approximate=True).astype(jnp.bfloat16)
                part = jnp.einsum(
                    "tsh,shd->td", activated, bank[1], preferred_element_type=jnp.float32
                )
            else:
                fc_rows = bank[0].reshape(-1, both.shape[2])
                proj_rows = bank[1].reshape(-1, both.shape[2])
                inner = lax.dot_general(
                    rows_in, fc_rows, (((1,), (1,)), ((), ())), preferred_element_type=jnp.float32
                )
                activated = jax.nn.gelu(inner, approximate=True).astype(jnp.bfloat16)
                part = jnp.dot(activated, proj_rows, preferred_element_type=jnp.float32)
            total = part if total is None else total + part
        return total

    returned = []
    for shift in range(1, group_count):
        there = [(g, (g + shift) % group_count) for g in range(group_count)]
        back = [(g, (g - shift) % group_count) for g in range(group_count)]
        partner_normed = lax.ppermute(normed, "group", there)
        partner_feed = feed(partner_normed).astype(jnp.bfloat16)
        returned.append(lax.ppermute(partner_feed, "group", back))
    summed = lax.optimization_barrier(residual + feed(normed))
    for part in returned:
        summed = summed + part.astype(jnp.float32)
    live = positions[:, None] < my_length
    return jnp.where(live, summed, 0.0).astype(jnp.bfloat16)[None]


def solution(mesh):
    return jax.shard_map(
        functools.partial(per_device, plan_ring(mesh)),
        mesh=mesh,
        in_specs=(
            P("group", "dev", None),
            P("group", "dev", None),
            P("group", "dev", None),
            P("group", "dev", None),
            P("group", "dev", None),
            P(),
            P(),
            P(None, ("group", "dev")),
            P(("group", "dev"), None),
            P("group", None),
            P("group", None),
            P("group", None),
            P("group", None),
        ),
        out_specs=P("group", "dev", None),
        check_vma=False,
    )
```
